128 devices in a mesh: req: 8 (over x, core), seq: 16 (over z, y).
Axes of the slice: x: 4, y: 4, z: 4, core: 2. Of those that a mesh axis runs over, the one named last changes fastest.
Arguments:
- hidden: bfloat16 [8, 2048, 2048], P('req', 'seq'), may hold values from -6 to 6
- lengths: int32 [8], replicated, may hold values from 1 to 2048, 10240 in all
- slot_request: int32 [8], replicated, may hold values from 0 to 7, each once
- norm_gain: bfloat16 [2048], replicated, may hold values from 0.099609375 to 1.8984375
- in_weight: bfloat16 [2, 2048, 4096], P(None, 'req', 'seq'), may hold values from -0.125 to 0.125
- conv_weight: bfloat16 [4, 4096], P(None, 'seq'), may hold values from -3 to 3
- conv_bias: bfloat16 [4096], P('seq'), may hold values from -0.5 to 0.5
- xproj_weight: bfloat16 [4096, 160], P('seq'), may hold values from -0.09375 to 0.09375
- dt_weight: bfloat16 [128, 4096], P(None, 'seq'), may hold values from -0.5 to 0.5
- dt_bias: bfloat16 [4096], P('seq'), may hold values from -6.91 to -2.25
- a_log: float32 [16, 4096], replicated, may hold values from -2.3 to 1.39
- skip_gain: float32 [4096], replicated, may hold values from 0.5 to 1.5
- out_weight: bfloat16 [4096, 2048], P('seq', 'req'), may hold values from -0.09375 to 0.09375
Outputs:
- mixed: bfloat16 [8, 2048, 2048], P('req', 'seq')
- final_state: float32 [8, 16, 4096], P('req', None, 'seq')
The draws below stay inside these ranges and needn't reach their ends.
Inputs may be any that keep to these rules, and one draw needn't show every extreme that they name: `lengths`: each slot's length is at least 1, the longest is exactly 2048, and they sum to 10240. `slot_request`: A permutation of the requests.
All inputs are finite; a program needn't handle non-finite values.
Results may differ from the reference program's by a relative error of at most 0.015.
Values may be sent and summed in bfloat16 or wider, within the bound.
No kernel may reach another device: no remote copies, remote signals or barrier semaphores. Data moves between devices by JAX's collectives and lax.ppermute only.
A program may use at most 128 MiB of HBM per device.

```python
import math
import jax
import jax.numpy as jnp
import numpy as np
from jax import lax

D = 2048
INNER = 4096
STATE = 16
RANK = 128
CONV = 4
LEN = 2048
REQS = 8


def draw_dt_bias(key, part):
    first, second, third = jax.random.split(key, 3)
    share = 0.5
    slow = jax.random.uniform(first, (INNER,), jnp.float32) < share
    slow_rate = jnp.exp(jax.random.uniform(second, (INNER,), jnp.float32, math.log(0.001), math.log(0.005)))
    fast_rate = jnp.exp(jax.random.uniform(third, (INNER,), jnp.float32, math.log(0.01), math.log(0.1)))
    rate = jnp.where(slow, slow_rate, fast_rate)
    return jnp.log(jnp.expm1(rate)).astype(jnp.bfloat16)


def block_scale(own_key, extent, shards, low, high):
    gain = 1.0
    for dim, parts in shards:
        steps = jax.random.uniform(jax.random.fold_in(jax.random.fold_in(own_key, 6), dim), (parts,), jnp.float32, low / len(shards), high / len(shards))
        gain = gain * jnp.repeat(jnp.exp(steps), extent[dim] // parts).reshape((-1,) + (1,) * (len(extent) - 1 - dim))
    return gain


def split_up(count, total, limit, skew):
    portions = [(1 << 20) // math.isqrt(grade ** skew) + 1 for grade in range(2, count + 1)]
    surplus, holding = total - limit - (count - 1), [1] * (count - 1)
    while surplus > 0:
        movable = [i for i in range(count - 1) if holding[i] < limit]
        whole, remaining = sum([portions[i] for i in movable]), surplus
        for i in movable:
            addition = min(limit - holding[i], max(1, remaining * portions[i] // whole), surplus)
            holding[i] = holding[i] + addition
            surplus = surplus - addition
    return np.array([limit] + holding)


def ragged(rng, count, total, reach, slope):
    if count == 2:
        one = jax.random.randint(rng, (), max(1, total - reach), min(reach, total - 1) + 1)
        return jnp.stack([one, total - one])
    tallies = jnp.asarray(split_up(count, total, reach, slope), jnp.int32)
    pairs = (count - 1) // 2
    giver, sink = tallies[1:1 + 2 * pairs:2], tallies[2:2 + 2 * pairs:2]
    margin = jnp.minimum(giver - 1, reach - sink)
    shifted = jax.random.randint(jax.random.fold_in(rng, 1), (pairs,), 0, 1 << 20) % (margin + 1)
    tallies = tallies.at[1:1 + 2 * pairs:2].set(giver - shifted).at[2:2 + 2 * pairs:2].set(sink + shifted)
    return tallies[jax.random.permutation(jax.random.fold_in(rng, 2), count)]


def bell_draw(key, dims, spread, bound, pieces=(), kind=jnp.bfloat16):
    loudness = block_scale(key, dims, pieces, -0.22, 0.18) if pieces else 1.0
    drawn = jax.random.normal(key, dims, jnp.float32) * spread * loudness
    return jnp.minimum(jnp.maximum(drawn, -bound), bound).astype(kind)


def setup_inputs(seed: int = 0) -> dict:
    arg_keys = jax.random.split(jax.random.key(seed), 14)
    hidden = bell_draw(arg_keys[0], (REQS, LEN, D), 1.0, 6.0, ((0, 8), (1, 16)))
    lengths = ragged(arg_keys[1], REQS, 5 * REQS * LEN // 8, LEN, 2).astype(jnp.int32)
    slot_request = jax.random.permutation(arg_keys[2], REQS).astype(jnp.int32)
    norm_gain = jnp.clip(1.0 + 0.18 * jax.random.normal(arg_keys[3], (D,), jnp.float32), 0.099609375, 1.8984375).astype(jnp.bfloat16)
    in_weight = bell_draw(arg_keys[4], (2, D, INNER), D ** -0.5, 0.125, ((1, 8), (2, 16)))
    conv_weight = bell_draw(arg_keys[5], (CONV, INNER), CONV ** -0.5, 3.0, ((1, 16),))
    conv_bias = jnp.clip(jax.random.uniform(arg_keys[6], (INNER,), jnp.float32, -0.5, 0.5) * block_scale(arg_keys[6], (INNER,), ((0, 16),), -0.4, 0.0), -0.5, 0.5).astype(jnp.bfloat16)
    xproj_weight = bell_draw(arg_keys[7], (INNER, RANK + 2 * STATE), INNER ** -0.5, 0.09375, ((0, 16),))
    dt_weight = bell_draw(arg_keys[8], (RANK, INNER), RANK ** -0.5, 0.5, ((1, 16),))
    dt_bias = draw_dt_bias(jax.random.fold_in(arg_keys[13], 71), 0)
    a_log = jnp.clip(jax.random.uniform(arg_keys[10], (STATE, INNER), jnp.float32, -2.3, 1.39), -2.3, 1.39)
    skip_gain = jnp.clip(jax.random.uniform(arg_keys[11], (INNER,), jnp.float32, 0.5, 1.5), 0.5, 1.5)
    out_weight = bell_draw(arg_keys[12], (INNER, D), INNER ** -0.5, 0.09375, ((0, 16), (1, 8)))
    return {"hidden": hidden, "lengths": lengths, "slot_request": slot_request, "norm_gain": norm_gain, "in_weight": in_weight, "conv_weight": conv_weight, "conv_bias": conv_bias, "xproj_weight": xproj_weight, "dt_weight": dt_weight, "dt_bias": dt_bias, "a_log": a_log, "skip_gain": skip_gain, "out_weight": out_weight}


def reference(hidden, lengths, slot_request, norm_gain, in_weight, conv_weight, conv_bias, xproj_weight, dt_weight, dt_bias, a_log, skip_gain, out_weight):
    tokens = hidden.astype(jnp.float32)
    scale = lax.rsqrt(lax.optimization_barrier(jnp.mean(tokens * tokens, axis=-1, keepdims=True)) + 1e-05)
    normed = (tokens * scale * norm_gain.astype(jnp.float32)).astype(jnp.bfloat16)
    flat = normed.reshape(REQS * LEN, D)
    xin = jnp.dot(flat, in_weight[0], preferred_element_type=jnp.float32).reshape(REQS, LEN, INNER)
    zgate = jnp.dot(flat, in_weight[1], preferred_element_type=jnp.float32).astype(jnp.bfloat16).reshape(REQS, LEN, INNER)
    padded = jnp.pad(xin, ((0, 0), (CONV - 1, 0), (0, 0)))
    taps = conv_weight.astype(jnp.float32)
    convolved = conv_bias.astype(jnp.float32) + jnp.zeros_like(xin)
    for tap in range(CONV):
        convolved = convolved + taps[tap] * padded[:, tap:tap + LEN, :]
    inner = jax.nn.silu(convolved).astype(jnp.bfloat16)
    proj = jnp.dot(inner.reshape(REQS * LEN, INNER), xproj_weight, preferred_element_type=jnp.float32)
    rate_low = proj[:, :RANK].astype(jnp.bfloat16)
    entry = proj[:, RANK:RANK + STATE].reshape(REQS, LEN, STATE)
    readout = proj[:, RANK + STATE:].reshape(REQS, LEN, STATE)
    live = (jnp.arange(LEN, dtype=jnp.int32)[None, :] < lengths[:, None]).astype(jnp.float32)
    delta = jax.nn.softplus(jnp.dot(rate_low, dt_weight, preferred_element_type=jnp.float32) + dt_bias.astype(jnp.float32))
    delta = delta.reshape(REQS, LEN, INNER) * live[:, :, None]
    decay = -jnp.exp(a_log)
    inner_f = inner.astype(jnp.float32)

    def advance(state, items):
        rate, value, into, outof = items
        state = jnp.exp(rate[:, None, :] * decay[None]) * state + (rate * value)[:, None, :] * into[:, :, None]
        result = lax.optimization_barrier(jnp.sum(outof[:, :, None] * state, axis=1)) + skip_gain * value
        return (state, result)
    moved = (jnp.swapaxes(delta, 0, 1), jnp.swapaxes(inner_f, 0, 1), jnp.swapaxes(entry, 0, 1), jnp.swapaxes(readout, 0, 1))
    start = jnp.zeros((REQS, STATE, INNER), jnp.float32)
    last, results = lax.scan(advance, start, moved)
    scanned = jnp.swapaxes(results, 0, 1).astype(jnp.bfloat16)
    gated = (scanned.astype(jnp.float32) * jax.nn.silu(zgate.astype(jnp.float32))).astype(jnp.bfloat16)
    branch = jnp.dot(gated.reshape(REQS * LEN, INNER), out_weight, preferred_element_type=jnp.float32).reshape(REQS, LEN, D)
    mixed = (tokens + branch).astype(jnp.bfloat16)
    final_state = jnp.zeros_like(last).at[slot_request].set(last)
    return (mixed, final_state)
```

```python
import jax
import jax.numpy as jnp
from jax import lax
from jax.sharding import PartitionSpec as P

STATE = 16
RANK = 128


def gather_a2a(block, axis, dim):
    count = lax.axis_size(axis)
    copies = jnp.broadcast_to(block[None], (count,) + block.shape)
    stacked = lax.all_to_all(copies, axis, split_axis=0, concat_axis=0, tiled=True)
    moved = jnp.moveaxis(stacked, 0, dim)
    shape = list(block.shape)
    shape[dim] = shape[dim] * count
    return moved.reshape(shape)


def to_blocks(array):
    pieces, length, columns = array.shape
    return jnp.moveaxis(array.reshape(pieces, 16, length // 16, columns), 1, 0)


def from_blocks(array):
    count, pieces, group, columns = array.shape
    return jnp.moveaxis(array, 0, 1).reshape(pieces, count * group, columns)


def piece_scan(rates, values, entry, readout, decay):
    pieces, length, columns = rates.shape
    group = length // 16
    positions = jnp.arange(length, dtype=jnp.int32)
    lower = (positions[None, :] <= positions[:, None]).astype(jnp.float32)
    running = jnp.einsum("rs,psw->prw", lower, rates, precision=lax.Precision.HIGHEST)

    def advance(state, items):
        rate, value, into, outof = items
        outputs = []
        for place in range(group):
            factor = jnp.exp(rate[:, place][:, None, :] * decay[None])
            state = (
                factor * state
                + (rate[:, place] * value[:, place])[:, None, :] * into[:, place][:, :, None]
            )
            outputs.append(jnp.sum(outof[:, place][:, :, None] * state, axis=1))
        return (state, jnp.stack(outputs, axis=1))

    start = jnp.zeros((pieces, decay.shape[0], columns), jnp.float32)
    end_local, local_out = lax.scan(
        advance, start, (to_blocks(rates), to_blocks(values), to_blocks(entry), to_blocks(readout))
    )
    total_decay = jnp.exp(running[:, length - 1][:, None, :] * decay[None])
    return (end_local, from_blocks(local_out), total_decay, running)


def carried_part(running, readout, decay, carry_in):

    def correct(items):
        total, outof = items
        kept = jnp.exp(total[:, :, None, :] * decay[None, None]) * carry_in[:, None]
        return jnp.sum(outof[:, :, :, None] * kept, axis=2)

    return from_blocks(lax.map(correct, (to_blocks(running), to_blocks(readout))))


def per_device(
    hidden,
    lengths,
    slot_request,
    norm_gain,
    in_weight,
    conv_weight,
    conv_bias,
    xproj_weight,
    dt_weight,
    dt_bias,
    a_log,
    skip_gain,
    out_weight,
):
    seq_count = lax.axis_size("seq")
    seq_index = lax.axis_index("seq")
    req_index = lax.axis_index("req")
    rows = hidden.shape[1]
    span = rows * seq_count
    width = in_weight.shape[2]
    taps_count = conv_weight.shape[0]
    state_count = a_log.shape[0]
    tokens = hidden[0].astype(jnp.float32)
    scale = lax.rsqrt(jnp.mean(tokens * tokens, axis=-1, keepdims=True) + 1e-05)
    normed = (tokens * scale * norm_gain.astype(jnp.float32)).astype(jnp.bfloat16)
    w_in = gather_a2a(in_weight, "req", 1)
    w_flat = jnp.concatenate((w_in[0], w_in[1]), axis=1)
    both = jnp.dot(
        lax.all_gather(normed, "seq", axis=0, tiled=True),
        w_flat,
        preferred_element_type=jnp.float32,
    )
    xin = both[:, :width]
    zgate = both[:, width:].astype(jnp.bfloat16)
    padded = jnp.pad(xin, ((taps_count - 1, 0), (0, 0)))
    taps = conv_weight.astype(jnp.float32)
    convolved = conv_bias.astype(jnp.float32) + jnp.zeros_like(xin)
    for tap in range(taps_count):
        convolved = convolved + taps[tap] * padded[tap : tap + span, :]
    inner = jax.nn.silu(convolved).astype(jnp.bfloat16)
    inner_tok = lax.all_to_all(inner, "seq", split_axis=0, concat_axis=1, tiled=True)
    xproj_full = gather_a2a(xproj_weight, "seq", 0)
    dt_full = gather_a2a(dt_weight, "seq", 1)
    dt_bias_full = gather_a2a(dt_bias, "seq", 0)
    proj = jnp.dot(inner_tok, xproj_full, preferred_element_type=jnp.float32)
    length_here = lax.dynamic_index_in_dim(lengths, req_index, 0, keepdims=False)
    positions = seq_index * rows + jnp.arange(rows, dtype=jnp.int32)
    live = (positions < length_here).astype(jnp.float32)
    rate_low = proj[:, :RANK].astype(jnp.bfloat16)
    delta_tok = (
        jax.nn.softplus(
            jnp.dot(rate_low, dt_full, preferred_element_type=jnp.float32)
            + dt_bias_full.astype(jnp.float32)
        )
        * live[:, None]
    )
    w_out = gather_a2a(out_weight, "req", 1)
    decay = -jnp.exp(a_log)
    inner_f = inner_tok.astype(jnp.float32)
    entry = proj[None, :, RANK : RANK + STATE]
    readout = proj[None, :, RANK + STATE :]
    end_local, local_out, total_decay, running = piece_scan(
        delta_tok[None], inner_f[None], entry, readout, decay
    )
    pair = jnp.stack((total_decay[0], end_local[0])).reshape(2, state_count, seq_count, width)
    pair_ch = lax.all_to_all(pair, "seq", split_axis=2, concat_axis=2, tiled=True)
    carry = jnp.zeros((state_count, width), jnp.float32)
    carries = []
    for block in range(seq_count):
        carries.append(carry)
        carry = pair_ch[0, :, block] * carry + pair_ch[1, :, block]
    carry_ch = jnp.stack(carries, axis=1)
    carry_in = lax.all_to_all(carry_ch, "seq", split_axis=1, concat_axis=1, tiled=True).reshape(
        state_count, seq_count * width
    )
    carried = carried_part(running, readout, decay, carry_in[None])
    scanned = ((local_out + carried)[0] + skip_gain * inner_f).astype(jnp.bfloat16)
    scanned_ch = lax.all_to_all(scanned, "seq", split_axis=1, concat_axis=0, tiled=True)
    gated_ch = (scanned_ch.astype(jnp.float32) * jax.nn.silu(zgate.astype(jnp.float32))).astype(
        jnp.bfloat16
    )
    branch = lax.psum_scatter(
        jnp.dot(gated_ch, w_out, preferred_element_type=jnp.float32).astype(jnp.bfloat16),
        "seq",
        scatter_dimension=0,
        tiled=True,
    ).astype(jnp.float32)
    slot_all = gather_a2a(carry[None], "req", 0)
    picked = (slot_request == req_index).astype(jnp.float32)
    final_state = jnp.sum(picked[:, None, None] * slot_all, axis=0, keepdims=True)
    mixed = (tokens + branch).astype(jnp.bfloat16)[None]
    return (mixed, final_state)


def solution(mesh):
    in_specs = (
        P("req", "seq", None),
        P(),
        P(),
        P(),
        P(None, "req", "seq"),
        P(None, "seq"),
        P("seq"),
        P("seq", None),
        P(None, "seq"),
        P("seq"),
        P(),
        P(),
        P("seq", "req"),
    )
    out_specs = (P("req", "seq", None), P("req", None, "seq"))
    return jax.shard_map(
        per_device, mesh=mesh, in_specs=in_specs, out_specs=out_specs, check_vma=False
    )
```

```python
import functools

import jax
import jax.numpy as jnp
from jax import lax
from jax.experimental import pallas as pl
from jax.experimental.pallas import tpu as pltpu
from jax.sharding import PartitionSpec as P

STATE = 16
RANK = 128


def gather_a2a(block, axis, dim):
    count = lax.axis_size(axis)
    copies = jnp.broadcast_to(block[None], (count,) + block.shape)
    stacked = lax.all_to_all(copies, axis, split_axis=0, concat_axis=0, tiled=True)
    moved = jnp.moveaxis(stacked, 0, dim)
    shape = list(block.shape)
    shape[dim] = shape[dim] * count
    return moved.reshape(shape)


LANES = 128
SUB = 8


def scan_body(emit, into_ref, outof_ref, rate_ref, value_ref, decay_ref, start_ref, skip_ref, *outs):
    steps = rate_ref.shape[0]
    states = decay_ref.shape[0]
    decay = [decay_ref[n] for n in range(states)]
    if emit:
        out_ref, = outs
        skip = skip_ref[...]
    else:
        end_ref, total_ref = outs

    def step(t, carry):
        held, acc = carry
        rate = rate_ref[t]
        value = value_ref[t]
        push = rate * value
        row = t * states
        new = []
        result = skip * value if emit else None
        for n in range(states):
            s = jnp.exp(rate * decay[n]) * held[n] + push * into_ref[row + n]
            if emit:
                result = result + outof_ref[row + n] * s
            new.append(s)
        if emit:
            out_ref[t] = result
        else:
            acc = acc + rate
        return (tuple(new), acc)

    held0 = tuple(start_ref[n] for n in range(states))
    acc0 = jnp.zeros((SUB, LANES), jnp.float32)
    held, acc = lax.fori_loop(0, steps, step, (held0, acc0))
    if not emit:
        for n in range(states):
            end_ref[n] = held[n]
            total_ref[n] = jnp.exp(acc * decay[n])


def run_scan(emit, into, outof, rate, value, decay, start, skip):
    steps, rows, lanes = rate.shape
    states = decay.shape[0]
    chunks = rows // SUB
    smem = pl.BlockSpec(memory_space=pltpu.MemorySpace.SMEM)
    seq_spec = pl.BlockSpec((steps, SUB, lanes), lambda i: (0, i, 0))
    st_spec = pl.BlockSpec((states, SUB, lanes), lambda i: (0, i, 0))
    skip_spec = pl.BlockSpec((SUB, lanes), lambda i: (i, 0))
    if emit:
        out_shape = jax.ShapeDtypeStruct((steps, rows, lanes), jnp.float32)
        out_specs = seq_spec
    else:
        out_shape = (jax.ShapeDtypeStruct((states, rows, lanes), jnp.float32),) * 2
        out_specs = (st_spec, st_spec)
    flops = steps * rows * lanes * states * 6
    return pl.pallas_call(
        functools.partial(scan_body, emit),
        grid=(chunks,),
        in_specs=[smem, smem, seq_spec, seq_spec, st_spec, st_spec, skip_spec],
        out_specs=out_specs,
        out_shape=out_shape,
        cost_estimate=pl.CostEstimate(
            flops=flops,
            transcendentals=steps * rows * lanes * states,
            bytes_accessed=(3 if emit else 2) * steps * rows * lanes * 4,
        ),
    )(into, outof, rate, value, decay, start, skip)


def per_device(
    hidden,
    lengths,
    slot_request,
    norm_gain,
    in_weight,
    conv_weight,
    conv_bias,
    xproj_weight,
    dt_weight,
    dt_bias,
    a_log,
    skip_gain,
    out_weight,
):
    seq_count = lax.axis_size("seq")
    seq_index = lax.axis_index("seq")
    req_index = lax.axis_index("req")
    rows = hidden.shape[1]
    span = rows * seq_count
    width = in_weight.shape[2]
    taps_count = conv_weight.shape[0]
    state_count = a_log.shape[0]
    total_inner = a_log.shape[1]
    tokens = hidden[0].astype(jnp.float32)
    scale = lax.rsqrt(jnp.mean(tokens * tokens, axis=-1, keepdims=True) + 1e-05)
    normed = (tokens * scale * norm_gain.astype(jnp.float32)).astype(jnp.bfloat16)
    w_in = gather_a2a(in_weight, "req", 1)
    w_flat = jnp.concatenate((w_in[0], w_in[1]), axis=1)
    both = jnp.dot(
        lax.all_gather(normed, "seq", axis=0, tiled=True),
        w_flat,
        preferred_element_type=jnp.float32,
    )
    xin = both[:, :width]
    zgate = both[:, width:].astype(jnp.bfloat16)
    padded = jnp.pad(xin, ((taps_count - 1, 0), (0, 0)))
    taps = conv_weight.astype(jnp.float32)
    convolved = conv_bias.astype(jnp.float32) + jnp.zeros_like(xin)
    for tap in range(taps_count):
        convolved = convolved + taps[tap] * padded[tap : tap + span, :]
    inner = jax.nn.silu(convolved).astype(jnp.bfloat16)
    inner_tok = lax.all_to_all(inner, "seq", split_axis=0, concat_axis=1, tiled=True)
    xproj_full = gather_a2a(xproj_weight, "seq", 0)
    dt_full = gather_a2a(dt_weight, "seq", 1)
    dt_bias_full = gather_a2a(dt_bias, "seq", 0)
    proj = jnp.dot(inner_tok, xproj_full, preferred_element_type=jnp.float32)
    length_here = lax.dynamic_index_in_dim(lengths, req_index, 0, keepdims=False)
    positions = seq_index * rows + jnp.arange(rows, dtype=jnp.int32)
    live = (positions < length_here).astype(jnp.float32)
    rate_low = proj[:, :RANK].astype(jnp.bfloat16)
    delta_tok = (
        jax.nn.softplus(
            jnp.dot(rate_low, dt_full, preferred_element_type=jnp.float32)
            + dt_bias_full.astype(jnp.float32)
        )
        * live[:, None]
    )
    w_out = gather_a2a(out_weight, "req", 1)
    decay = -jnp.exp(a_log)
    lanes = 128
    groups = total_inner // lanes
    inner_f = inner_tok.astype(jnp.float32)
    into = proj[:, RANK : RANK + STATE].reshape(-1)
    outof = proj[:, RANK + STATE :].reshape(-1)
    rate_l = delta_tok.reshape(rows, groups, lanes)
    value_l = inner_f.reshape(rows, groups, lanes)
    decay_l = decay.reshape(state_count, groups, lanes)
    skip_l = skip_gain.reshape(groups, lanes)
    end_l, total_l = run_scan(
        False, into, outof, rate_l, value_l, decay_l,
        jnp.zeros((state_count, groups, lanes), jnp.float32), skip_l,
    )
    pair = jnp.stack(
        (total_l.reshape(state_count, total_inner), end_l.reshape(state_count, total_inner))
    ).reshape(2, state_count, seq_count, width)
    pair_ch = lax.all_to_all(pair, "seq", split_axis=2, concat_axis=2, tiled=True)
    carry = jnp.zeros((state_count, width), jnp.float32)
    carries = []
    for block in range(seq_count):
        carries.append(carry)
        carry = pair_ch[0, :, block] * carry + pair_ch[1, :, block]
    carry_ch = jnp.stack(carries, axis=1)
    carry_in = lax.all_to_all(carry_ch, "seq", split_axis=1, concat_axis=1, tiled=True)
    out_l = run_scan(
        True, into, outof, rate_l, value_l, decay_l,
        carry_in.reshape(state_count, groups, lanes), skip_l,
    )
    scanned = out_l.reshape(rows, total_inner).astype(jnp.bfloat16)
    scanned_ch = lax.all_to_all(scanned, "seq", split_axis=1, concat_axis=0, tiled=True)
    gated_ch = (scanned_ch.astype(jnp.float32) * jax.nn.silu(zgate.astype(jnp.float32))).astype(
        jnp.bfloat16
    )
    branch = lax.psum_scatter(
        jnp.dot(gated_ch, w_out, preferred_element_type=jnp.float32).astype(jnp.bfloat16),
        "seq",
        scatter_dimension=0,
        tiled=True,
    ).astype(jnp.float32)
    slot_all = gather_a2a(carry[None], "req", 0)
    picked = (slot_request == req_index).astype(jnp.float32)
    final_state = jnp.sum(picked[:, None, None] * slot_all, axis=0, keepdims=True)
    mixed = (tokens + branch).astype(jnp.bfloat16)[None]
    return (mixed, final_state)


def solution(mesh):
    in_specs = (
        P("req", "seq", None),
        P(),
        P(),
        P(),
        P(None, "req", "seq"),
        P(None, "seq"),
        P("seq"),
        P("seq", None),
        P(None, "seq"),
        P("seq"),
        P(),
        P(),
        P("seq", "req"),
    )
    out_specs = (P("req", "seq", None), P("req", None, "seq"))
    return jax.shard_map(
        per_device, mesh=mesh, in_specs=in_specs, out_specs=out_specs, check_vma=False
    )
```

```python
import functools

import jax
import jax.numpy as jnp
from jax import lax
from jax.experimental import pallas as pl
from jax.experimental.pallas import tpu as pltpu
from jax.sharding import Mesh, PartitionSpec as P

STATE = 16
RANK = 128


def gather_a2a(block, axis, dim):
    count = lax.axis_size(axis)
    copies = jnp.broadcast_to(block[None], (count,) + block.shape)
    stacked = lax.all_to_all(copies, axis, split_axis=0, concat_axis=0, tiled=True)
    moved = jnp.moveaxis(stacked, 0, dim)
    shape = list(block.shape)
    shape[dim] = shape[dim] * count
    return moved.reshape(shape)


LANES = 128
SUB = 8


def scan_body(emit, into_ref, outof_ref, rate_ref, value_ref, decay_ref, start_ref, skip_ref, *outs):
    steps = rate_ref.shape[0]
    states = decay_ref.shape[0]
    decay = [decay_ref[n] for n in range(states)]
    if emit:
        out_ref, = outs
        skip = skip_ref[...]
    else:
        end_ref, total_ref = outs

    def step(t, carry):
        held, acc = carry
        rate = rate_ref[t]
        value = value_ref[t]
        push = rate * value
        row = t * states
        new = []
        result = skip * value if emit else None
        for n in range(states):
            s = jnp.exp(rate * decay[n]) * held[n] + push * into_ref[row + n]
            if emit:
                result = result + outof_ref[row + n] * s
            new.append(s)
        if emit:
            out_ref[t] = result
        else:
            acc = acc + rate
        return (tuple(new), acc)

    held0 = tuple(start_ref[n] for n in range(states))
    acc0 = jnp.zeros((SUB, LANES), jnp.float32)
    held, acc = lax.fori_loop(0, steps, step, (held0, acc0))
    if not emit:
        for n in range(states):
            end_ref[n] = held[n]
            total_ref[n] = jnp.exp(acc * decay[n])


def run_scan(emit, into, outof, rate, value, decay, start, skip):
    steps, rows, lanes = rate.shape
    states = decay.shape[0]
    chunks = rows // SUB
    smem = pl.BlockSpec(memory_space=pltpu.MemorySpace.SMEM)
    seq_spec = pl.BlockSpec((steps, SUB, lanes), lambda i: (0, i, 0))
    st_spec = pl.BlockSpec((states, SUB, lanes), lambda i: (0, i, 0))
    skip_spec = pl.BlockSpec((SUB, lanes), lambda i: (i, 0))
    if emit:
        out_shape = jax.ShapeDtypeStruct((steps, rows, lanes), jnp.float32)
        out_specs = seq_spec
    else:
        out_shape = (jax.ShapeDtypeStruct((states, rows, lanes), jnp.float32),) * 2
        out_specs = (st_spec, st_spec)
    flops = steps * rows * lanes * states * 6
    return pl.pallas_call(
        functools.partial(scan_body, emit),
        grid=(chunks,),
        in_specs=[smem, smem, seq_spec, seq_spec, st_spec, st_spec, skip_spec],
        out_specs=out_specs,
        out_shape=out_shape,
        cost_estimate=pl.CostEstimate(
            flops=flops,
            transcendentals=steps * rows * lanes * states,
            bytes_accessed=(3 if emit else 2) * steps * rows * lanes * 4,
        ),
    )(into, outof, rate, value, decay, start, skip)


def per_device(
    hidden,
    lengths,
    slot_request,
    norm_gain,
    in_weight,
    conv_weight,
    conv_bias,
    xproj_weight,
    dt_weight,
    dt_bias,
    a_log,
    skip_gain,
    out_weight,
):
    seq = ("sz", "sy")
    rows_n = lax.axis_size("sz")
    cols_n = lax.axis_size("sy")
    seq_count = rows_n * cols_n
    seq_index = lax.axis_index(seq)
    req_index = lax.axis_index("req")
    rows = hidden.shape[1]
    span = rows * seq_count
    width = in_weight.shape[2]
    taps_count = conv_weight.shape[0]
    state_count = a_log.shape[0]
    total_inner = a_log.shape[1]
    model = hidden.shape[2]
    w_in = gather_a2a(in_weight, "req", 1)
    w_out = gather_a2a(out_weight, "req", 1)
    xproj_full = gather_a2a(xproj_weight, seq, 0)
    dt_full = gather_a2a(dt_weight, seq, 1)
    dt_bias_full = gather_a2a(dt_bias, seq, 0)
    w_col = lax.all_gather(w_out, "sz", axis=0, tiled=False)
    w_in, w_col, xproj_full, dt_full, dt_bias_full = lax.optimization_barrier(
        (w_in, w_col, xproj_full, dt_full, dt_bias_full)
    )
    tokens = hidden[0].astype(jnp.float32)
    scale = lax.rsqrt(jnp.mean(tokens * tokens, axis=-1, keepdims=True) + 1e-05)
    normed = (tokens * scale * norm_gain.astype(jnp.float32)).astype(jnp.bfloat16)
    w_flat = jnp.concatenate((w_in[0], w_in[1]), axis=1)
    both = jnp.dot(
        lax.all_gather(normed, seq, axis=0, tiled=True),
        w_flat,
        preferred_element_type=jnp.float32,
    )
    xin = both[:, :width]
    zgate = both[:, width:].astype(jnp.bfloat16)
    z_grid = lax.all_to_all(
        zgate.reshape(rows_n, span // rows_n, width), "sz", split_axis=0, concat_axis=0, tiled=True
    )
    padded = jnp.pad(xin, ((taps_count - 1, 0), (0, 0)))
    taps = conv_weight.astype(jnp.float32)
    convolved = conv_bias.astype(jnp.float32) + jnp.zeros_like(xin)
    for tap in range(taps_count):
        convolved = convolved + taps[tap] * padded[tap : tap + span, :]
    inner = jax.nn.silu(convolved).astype(jnp.bfloat16)
    inner_tok = lax.all_to_all(inner, seq, split_axis=0, concat_axis=1, tiled=True)
    proj = jnp.dot(inner_tok, xproj_full, preferred_element_type=jnp.float32)
    length_here = lax.dynamic_index_in_dim(lengths, req_index, 0, keepdims=False)
    positions = seq_index * rows + jnp.arange(rows, dtype=jnp.int32)
    live = (positions < length_here).astype(jnp.float32)
    rate_low = proj[:, :RANK].astype(jnp.bfloat16)
    delta_tok = (
        jax.nn.softplus(
            jnp.dot(rate_low, dt_full, preferred_element_type=jnp.float32)
            + dt_bias_full.astype(jnp.float32)
        )
        * live[:, None]
    )
    decay = -jnp.exp(a_log)
    lanes = 128
    groups = total_inner // lanes
    inner_f = inner_tok.astype(jnp.float32)
    into = proj[:, RANK : RANK + STATE].reshape(-1)
    outof = proj[:, RANK + STATE :].reshape(-1)
    rate_l = delta_tok.reshape(rows, groups, lanes)
    value_l = inner_f.reshape(rows, groups, lanes)
    decay_l = decay.reshape(state_count, groups, lanes)
    skip_l = skip_gain.reshape(groups, lanes)
    end_l, total_l = run_scan(
        False, into, outof, rate_l, value_l, decay_l,
        jnp.zeros((state_count, groups, lanes), jnp.float32), skip_l,
    )
    pair = jnp.stack(
        (total_l.reshape(state_count, total_inner), end_l.reshape(state_count, total_inner))
    ).reshape(2, state_count, seq_count, width)
    pair_ch = lax.all_to_all(pair, seq, split_axis=2, concat_axis=2, tiled=True)
    carry = jnp.zeros((state_count, width), jnp.float32)
    carries = []
    for block in range(seq_count):
        carries.append(carry)
        carry = pair_ch[0, :, block] * carry + pair_ch[1, :, block]
    carry_ch = jnp.stack(carries, axis=1)
    carry_in = lax.all_to_all(carry_ch, seq, split_axis=1, concat_axis=1, tiled=True)
    out_l = run_scan(
        True, into, outof, rate_l, value_l, decay_l,
        carry_in.reshape(state_count, groups, lanes), skip_l,
    )
    scanned = out_l.reshape(rows, rows_n, cols_n, width).astype(jnp.bfloat16)
    scanned_grid = lax.all_to_all(scanned, "sy", split_axis=2, concat_axis=0, tiled=True)
    z_here = z_grid.reshape(rows_n, cols_n, rows, width).transpose(1, 2, 0, 3)
    gated = (
        scanned_grid.reshape(cols_n, rows, rows_n, width).astype(jnp.float32)
        * jax.nn.silu(z_here.astype(jnp.float32))
    ).astype(jnp.bfloat16)
    partial = jnp.einsum(
        "ktac,acd->ktd", gated, w_col, preferred_element_type=jnp.float32
    ).astype(jnp.bfloat16)
    branch = lax.psum_scatter(
        partial.reshape(cols_n * rows, model), "sy", scatter_dimension=0, tiled=True
    ).astype(jnp.float32)
    slot_all = gather_a2a(carry[None], "req", 0)
    picked = (slot_request == req_index).astype(jnp.float32)
    final_state = jnp.sum(picked[:, None, None] * slot_all, axis=0, keepdims=True)
    mixed = (tokens + branch).astype(jnp.bfloat16)[None]
    return (mixed, final_state)


def solution(mesh):
    seq_n = mesh.shape["seq"]
    rows_n = 1
    while rows_n * rows_n < seq_n:
        rows_n *= 2
    grid = Mesh(mesh.devices.reshape(mesh.shape["req"], rows_n, seq_n // rows_n), ("req", "sz", "sy"))
    seq = ("sz", "sy")
    in_specs = (
        P("req", seq, None),
        P(),
        P(),
        P(),
        P(None, "req", seq),
        P(None, seq),
        P(seq),
        P(seq, None),
        P(None, seq),
        P(seq),
        P(),
        P(),
        P(seq, "req"),
    )
    out_specs = (P("req", seq, None), P("req", None, seq))
    return jax.shard_map(
        per_device, mesh=grid, in_specs=in_specs, out_specs=out_specs, check_vma=False
    )
```

```python
import functools

import jax
import jax.numpy as jnp
from jax import lax
from jax.experimental import pallas as pl
from jax.experimental.pallas import tpu as pltpu
from jax.sharding import Mesh, PartitionSpec as P

STATE = 16
RANK = 128


def gather_a2a(block, axis, dim):
    count = lax.axis_size(axis)
    copies = jnp.broadcast_to(block[None], (count,) + block.shape)
    stacked = lax.all_to_all(copies, axis, split_axis=0, concat_axis=0, tiled=True)
    moved = jnp.moveaxis(stacked, 0, dim)
    shape = list(block.shape)
    shape[dim] = shape[dim] * count
    return moved.reshape(shape)


LANES = 128
SUB = 8


def scan_body(emit, into_ref, outof_ref, rate_ref, value_ref, decay_ref, start_ref, skip_ref, *outs):
    steps = rate_ref.shape[0]
    states = decay_ref.shape[0]
    decay = [decay_ref[n] for n in range(states)]
    if emit:
        out_ref, = outs
        skip = skip_ref[...]
    else:
        end_ref, total_ref = outs

    def step(t, carry):
        held, acc = carry
        rate = rate_ref[t]
        value = value_ref[t]
        push = rate * value
        row = t * states
        new = []
        result = skip * value if emit else None
        for n in range(states):
            s = jnp.exp(rate * decay[n]) * held[n] + push * into_ref[row + n]
            if emit:
                result = result + outof_ref[row + n] * s
            new.append(s)
        if emit:
            out_ref[t] = result
        else:
            acc = acc + rate
        return (tuple(new), acc)

    held0 = tuple(start_ref[n] for n in range(states))
    acc0 = jnp.zeros((SUB, LANES), jnp.float32)
    held, acc = lax.fori_loop(0, steps, step, (held0, acc0))
    if not emit:
        for n in range(states):
            end_ref[n] = held[n]
            total_ref[n] = jnp.exp(acc * decay[n])


def run_scan(emit, into, outof, rate, value, decay, start, skip):
    steps, rows, lanes = rate.shape
    states = decay.shape[0]
    chunks = rows // SUB
    smem = pl.BlockSpec(memory_space=pltpu.MemorySpace.SMEM)
    seq_spec = pl.BlockSpec((steps, SUB, lanes), lambda i: (0, i, 0))
    st_spec = pl.BlockSpec((states, SUB, lanes), lambda i: (0, i, 0))
    skip_spec = pl.BlockSpec((SUB, lanes), lambda i: (i, 0))
    if emit:
        out_shape = jax.ShapeDtypeStruct((steps, rows, lanes), jnp.float32)
        out_specs = seq_spec
    else:
        out_shape = (jax.ShapeDtypeStruct((states, rows, lanes), jnp.float32),) * 2
        out_specs = (st_spec, st_spec)
    flops = steps * rows * lanes * states * 6
    return pl.pallas_call(
        functools.partial(scan_body, emit),
        grid=(chunks,),
        in_specs=[smem, smem, seq_spec, seq_spec, st_spec, st_spec, skip_spec],
        out_specs=out_specs,
        out_shape=out_shape,
        cost_estimate=pl.CostEstimate(
            flops=flops,
            transcendentals=steps * rows * lanes * states,
            bytes_accessed=(3 if emit else 2) * steps * rows * lanes * 4,
        ),
    )(into, outof, rate, value, decay, start, skip)


def per_device(
    hidden,
    lengths,
    slot_request,
    norm_gain,
    in_weight,
    conv_weight,
    conv_bias,
    xproj_weight,
    dt_weight,
    dt_bias,
    a_log,
    skip_gain,
    out_weight,
):
    seq = ("sz", "sy")
    rows_n = lax.axis_size("sz")
    cols_n = lax.axis_size("sy")
    seq_count = rows_n * cols_n
    seq_index = lax.axis_index(seq)
    req_index = lax.axis_index("req")
    rows = hidden.shape[1]
    span = rows * seq_count
    width = in_weight.shape[2]
    taps_count = conv_weight.shape[0]
    state_count = a_log.shape[0]
    total_inner = a_log.shape[1]
    model = hidden.shape[2]
    w_in = gather_a2a(in_weight, "req", 1)
    tokens = hidden[0].astype(jnp.float32)
    scale = lax.rsqrt(jnp.mean(tokens * tokens, axis=-1, keepdims=True) + 1e-05)
    normed = (tokens * scale * norm_gain.astype(jnp.float32)).astype(jnp.bfloat16)
    half = model // 2
    normed_a = lax.all_gather(normed[:, :half], seq, axis=0, tiled=True)
    normed_b = gather_a2a(normed[:, half:], seq, 0)
    xproj_w, dt_w, dt_b, w_late, _, _ = lax.optimization_barrier(
        (xproj_weight, dt_weight, dt_bias, out_weight, normed_a, normed_b)
    )
    xproj_full = gather_a2a(xproj_w, seq, 0)
    dt_full = gather_a2a(dt_w, seq, 1)
    dt_bias_full = gather_a2a(dt_b, seq, 0)
    w_col = lax.all_gather(gather_a2a(w_late, "req", 1), "sz", axis=0, tiled=False)
    w_flat = jnp.concatenate((w_in[0], w_in[1]), axis=1)
    both = jnp.dot(normed_a, w_flat[:half], preferred_element_type=jnp.float32) + jnp.dot(
        normed_b, w_flat[half:], preferred_element_type=jnp.float32
    )
    xin = both[:, :width]
    zgate = both[:, width:].astype(jnp.bfloat16)
    z_grid = lax.all_to_all(
        zgate.reshape(rows_n, span // rows_n, width), "sz", split_axis=0, concat_axis=0, tiled=True
    )
    padded = jnp.pad(xin, ((taps_count - 1, 0), (0, 0)))
    taps = conv_weight.astype(jnp.float32)
    convolved = conv_bias.astype(jnp.float32) + jnp.zeros_like(xin)
    for tap in range(taps_count):
        convolved = convolved + taps[tap] * padded[tap : tap + span, :]
    inner = jax.nn.silu(convolved).astype(jnp.bfloat16)
    inner_tok = lax.all_to_all(inner, seq, split_axis=0, concat_axis=1, tiled=True)
    proj = jnp.dot(inner_tok, xproj_full, preferred_element_type=jnp.float32)
    length_here = lax.dynamic_index_in_dim(lengths, req_index, 0, keepdims=False)
    positions = seq_index * rows + jnp.arange(rows, dtype=jnp.int32)
    live = (positions < length_here).astype(jnp.float32)
    rate_low = proj[:, :RANK].astype(jnp.bfloat16)
    delta_tok = (
        jax.nn.softplus(
            jnp.dot(rate_low, dt_full, preferred_element_type=jnp.float32)
            + dt_bias_full.astype(jnp.float32)
        )
        * live[:, None]
    )
    decay = -jnp.exp(a_log)
    lanes = 128
    groups = total_inner // lanes
    inner_f = inner_tok.astype(jnp.float32)
    into = proj[:, RANK : RANK + STATE].reshape(-1)
    outof = proj[:, RANK + STATE :].reshape(-1)
    rate_l = delta_tok.reshape(rows, groups, lanes)
    value_l = inner_f.reshape(rows, groups, lanes)
    decay_l = decay.reshape(state_count, groups, lanes)
    skip_l = skip_gain.reshape(groups, lanes)
    end_l, total_l = run_scan(
        False, into, outof, rate_l, value_l, decay_l,
        jnp.zeros((state_count, groups, lanes), jnp.float32), skip_l,
    )
    pair = jnp.stack(
        (total_l.reshape(state_count, total_inner), end_l.reshape(state_count, total_inner))
    ).reshape(2, state_count, seq_count, width)
    pair_ch = lax.all_to_all(pair, seq, split_axis=2, concat_axis=2, tiled=True)
    carry = jnp.zeros((state_count, width), jnp.float32)
    carries = []
    for block in range(seq_count):
        carries.append(carry)
        carry = pair_ch[0, :, block] * carry + pair_ch[1, :, block]
    carry_ch = jnp.stack(carries, axis=1)
    carry_in = lax.all_to_all(carry_ch, seq, split_axis=1, concat_axis=1, tiled=True)
    out_l = run_scan(
        True, into, outof, rate_l, value_l, decay_l,
        carry_in.reshape(state_count, groups, lanes), skip_l,
    )
    scanned = out_l.reshape(rows, rows_n, cols_n, width).astype(jnp.bfloat16)
    scanned_grid = lax.all_to_all(scanned, "sy", split_axis=2, concat_axis=0, tiled=True)
    z_here = z_grid.reshape(rows_n, cols_n, rows, width).transpose(1, 2, 0, 3)
    gated = (
        scanned_grid.reshape(cols_n, rows, rows_n, width).astype(jnp.float32)
        * jax.nn.silu(z_here.astype(jnp.float32))
    ).astype(jnp.bfloat16)
    partial = jnp.einsum(
        "ktac,acd->ktd", gated, w_col, preferred_element_type=jnp.float32
    ).astype(jnp.bfloat16)
    branch = lax.psum_scatter(
        partial.reshape(cols_n * rows, model), "sy", scatter_dimension=0, tiled=True
    ).astype(jnp.float32)
    slot_all = gather_a2a(carry[None], "req", 0)
    picked = (slot_request == req_index).astype(jnp.float32)
    final_state = jnp.sum(picked[:, None, None] * slot_all, axis=0, keepdims=True)
    mixed = (tokens + branch).astype(jnp.bfloat16)[None]
    return (mixed, final_state)


def solution(mesh):
    seq_n = mesh.shape["seq"]
    rows_n = 1
    while rows_n * rows_n < seq_n:
        rows_n *= 2
    grid = Mesh(mesh.devices.reshape(mesh.shape["req"], rows_n, seq_n // rows_n), ("req", "sz", "sy"))
    seq = ("sz", "sy")
    in_specs = (
        P("req", seq, None),
        P(),
        P(),
        P(),
        P(None, "req", seq),
        P(None, seq),
        P(seq),
        P(seq, None),
        P(None, seq),
        P(seq),
        P(),
        P(),
        P(seq, "req"),
    )
    out_specs = (P("req", seq, None), P("req", None, seq))
    return jax.shard_map(
        per_device, mesh=grid, in_specs=in_specs, out_specs=out_specs, check_vma=False
    )
```

```python
import functools

import jax
import jax.numpy as jnp
from jax import lax
from jax.experimental import pallas as pl
from jax.experimental.pallas import tpu as pltpu
from jax.sharding import Mesh, PartitionSpec as P

STATE = 16
RANK = 128


def gather_a2a(block, axis, dim):
    count = lax.axis_size(axis)
    copies = jnp.broadcast_to(block[None], (count,) + block.shape)
    stacked = lax.all_to_all(copies, axis, split_axis=0, concat_axis=0, tiled=True)
    moved = jnp.moveaxis(stacked, 0, dim)
    shape = list(block.shape)
    shape[dim] = shape[dim] * count
    return moved.reshape(shape)


LANES = 128
SUB = 8


def scan_body(emit, into_ref, outof_ref, rate_ref, value_ref, decay_ref, start_ref, skip_ref, *outs):
    steps = rate_ref.shape[0]
    states = decay_ref.shape[0]
    decay = [decay_ref[n] for n in range(states)]
    if emit:
        out_ref, = outs
        skip = skip_ref[...]
    else:
        end_ref, total_ref = outs

    def step(t, carry):
        held, acc = carry
        rate = rate_ref[t]
        value = value_ref[t]
        push = rate * value
        row = t * states
        new = []
        result = skip * value if emit else None
        for n in range(states):
            s = jnp.exp(rate * decay[n]) * held[n] + push * into_ref[row + n]
            if emit:
                result = result + outof_ref[row + n] * s
            new.append(s)
        if emit:
            out_ref[t] = result
        else:
            acc = acc + rate
        return (tuple(new), acc)

    held0 = tuple(start_ref[n] for n in range(states))
    acc0 = jnp.zeros((SUB, LANES), jnp.float32)
    held, acc = lax.fori_loop(0, steps, step, (held0, acc0))
    if not emit:
        for n in range(states):
            end_ref[n] = held[n]
            total_ref[n] = jnp.exp(acc * decay[n])


def run_scan(emit, into, outof, rate, value, decay, start, skip):
    steps, rows, lanes = rate.shape
    states = decay.shape[0]
    chunks = rows // SUB
    smem = pl.BlockSpec(memory_space=pltpu.MemorySpace.SMEM)
    seq_spec = pl.BlockSpec((steps, SUB, lanes), lambda i: (0, i, 0))
    st_spec = pl.BlockSpec((states, SUB, lanes), lambda i: (0, i, 0))
    skip_spec = pl.BlockSpec((SUB, lanes), lambda i: (i, 0))
    if emit:
        out_shape = jax.ShapeDtypeStruct((steps, rows, lanes), jnp.float32)
        out_specs = seq_spec
    else:
        out_shape = (jax.ShapeDtypeStruct((states, rows, lanes), jnp.float32),) * 2
        out_specs = (st_spec, st_spec)
    flops = steps * rows * lanes * states * 6
    return pl.pallas_call(
        functools.partial(scan_body, emit),
        grid=(chunks,),
        in_specs=[smem, smem, seq_spec, seq_spec, st_spec, st_spec, skip_spec],
        out_specs=out_specs,
        out_shape=out_shape,
        cost_estimate=pl.CostEstimate(
            flops=flops,
            transcendentals=steps * rows * lanes * states,
            bytes_accessed=(3 if emit else 2) * steps * rows * lanes * 4,
        ),
    )(into, outof, rate, value, decay, start, skip)


def per_device(
    hidden,
    lengths,
    slot_request,
    norm_gain,
    in_weight,
    conv_weight,
    conv_bias,
    xproj_weight,
    dt_weight,
    dt_bias,
    a_log,
    skip_gain,
    out_weight,
):
    seq = ("sz", "sy")
    rows_n = lax.axis_size("sz")
    cols_n = lax.axis_size("sy")
    seq_count = rows_n * cols_n
    seq_index = lax.axis_index(seq)
    req_index = lax.axis_index("req")
    rows = hidden.shape[1]
    span = rows * seq_count
    width = in_weight.shape[2]
    taps_count = conv_weight.shape[0]
    state_count = a_log.shape[0]
    total_inner = a_log.shape[1]
    model = hidden.shape[2]
    tokens = hidden[0].astype(jnp.float32)
    scale = lax.rsqrt(jnp.mean(tokens * tokens, axis=-1, keepdims=True) + 1e-05)
    normed = (tokens * scale * norm_gain.astype(jnp.float32)).astype(jnp.bfloat16)
    normed_all = lax.all_gather(normed, seq, axis=0, tiled=True)
    w_in = gather_a2a(in_weight, "req", 1)
    xproj_w, dt_w, dt_b, _ = lax.optimization_barrier((xproj_weight, dt_weight, dt_bias, normed))
    xproj_full = gather_a2a(xproj_w, seq, 0)
    dt_full = gather_a2a(dt_w, seq, 1)
    dt_bias_full = gather_a2a(dt_b, seq, 0)
    w_in, xproj_full, dt_full, dt_bias_full = lax.optimization_barrier(
        (w_in, xproj_full, dt_full, dt_bias_full)
    )
    w_late, _ = lax.optimization_barrier((out_weight, normed_all))
    w_col = lax.all_gather(gather_a2a(w_late, "req", 1), "sz", axis=0, tiled=False)
    w_flat = jnp.concatenate((w_in[0], w_in[1]), axis=1)
    both = jnp.dot(normed_all, w_flat, preferred_element_type=jnp.float32)
    xin = both[:, :width]
    zgate = both[:, width:].astype(jnp.bfloat16)
    z_grid = lax.all_to_all(
        zgate.reshape(rows_n, span // rows_n, width), "sz", split_axis=0, concat_axis=0, tiled=True
    )
    padded = jnp.pad(xin, ((taps_count - 1, 0), (0, 0)))
    taps = conv_weight.astype(jnp.float32)
    convolved = conv_bias.astype(jnp.float32) + jnp.zeros_like(xin)
    for tap in range(taps_count):
        convolved = convolved + taps[tap] * padded[tap : tap + span, :]
    inner = jax.nn.silu(convolved).astype(jnp.bfloat16)
    inner_tok = lax.all_to_all(inner, seq, split_axis=0, concat_axis=1, tiled=True)
    proj = jnp.dot(inner_tok, xproj_full, preferred_element_type=jnp.float32)
    length_here = lax.dynamic_index_in_dim(lengths, req_index, 0, keepdims=False)
    positions = seq_index * rows + jnp.arange(rows, dtype=jnp.int32)
    live = (positions < length_here).astype(jnp.float32)
    rate_low = proj[:, :RANK].astype(jnp.bfloat16)
    delta_tok = (
        jax.nn.softplus(
            jnp.dot(rate_low, dt_full, preferred_element_type=jnp.float32)
            + dt_bias_full.astype(jnp.float32)
        )
        * live[:, None]
    )
    decay = -jnp.exp(a_log)
    lanes = 128
    groups = total_inner // lanes
    inner_f = inner_tok.astype(jnp.float32)
    into = proj[:, RANK : RANK + STATE].reshape(-1)
    outof = proj[:, RANK + STATE :].reshape(-1)
    rate_l = delta_tok.reshape(rows, groups, lanes)
    value_l = inner_f.reshape(rows, groups, lanes)
    decay_l = decay.reshape(state_count, groups, lanes)
    skip_l = skip_gain.reshape(groups, lanes)
    end_l, total_l = run_scan(
        False, into, outof, rate_l, value_l, decay_l,
        jnp.zeros((state_count, groups, lanes), jnp.float32), skip_l,
    )
    pair = jnp.stack(
        (total_l.reshape(state_count, total_inner), end_l.reshape(state_count, total_inner))
    ).reshape(2, state_count, seq_count, width)
    pair_ch = lax.all_to_all(pair, seq, split_axis=2, concat_axis=2, tiled=True)
    carry = jnp.zeros((state_count, width), jnp.float32)
    carries = []
    for block in range(seq_count):
        carries.append(carry)
        carry = pair_ch[0, :, block] * carry + pair_ch[1, :, block]
    carry_ch = jnp.stack(carries, axis=1)
    carry_in = lax.all_to_all(carry_ch, seq, split_axis=1, concat_axis=1, tiled=True)
    out_l = run_scan(
        True, into, outof, rate_l, value_l, decay_l,
        carry_in.reshape(state_count, groups, lanes), skip_l,
    )
    scanned = out_l.reshape(rows, rows_n, cols_n, width).astype(jnp.bfloat16)
    scanned_grid = lax.all_to_all(scanned, "sy", split_axis=2, concat_axis=0, tiled=True)
    z_here = z_grid.reshape(rows_n, cols_n, rows, width).transpose(1, 2, 0, 3)
    gated = (
        scanned_grid.reshape(cols_n, rows, rows_n, width).astype(jnp.float32)
        * jax.nn.silu(z_here.astype(jnp.float32))
    ).astype(jnp.bfloat16)
    partial = jnp.einsum(
        "ktac,acd->ktd", gated, w_col, preferred_element_type=jnp.float32
    ).astype(jnp.bfloat16)
    branch = lax.psum_scatter(
        partial.reshape(cols_n * rows, model), "sy", scatter_dimension=0, tiled=True
    ).astype(jnp.float32)
    slot_all = gather_a2a(carry[None], "req", 0)
    picked = (slot_request == req_index).astype(jnp.float32)
    final_state = jnp.sum(picked[:, None, None] * slot_all, axis=0, keepdims=True)
    mixed = (tokens + branch).astype(jnp.bfloat16)[None]
    return (mixed, final_state)


def solution(mesh):
    seq_n = mesh.shape["seq"]
    rows_n = 1
    while rows_n * rows_n < seq_n:
        rows_n *= 2
    grid = Mesh(mesh.devices.reshape(mesh.shape["req"], rows_n, seq_n // rows_n), ("req", "sz", "sy"))
    seq = ("sz", "sy")
    in_specs = (
        P("req", seq, None),
        P(),
        P(),
        P(),
        P(None, "req", seq),
        P(None, seq),
        P(seq),
        P(seq, None),
        P(None, seq),
        P(seq),
        P(),
        P(),
        P(seq, "req"),
    )
    out_specs = (P("req", seq, None), P("req", None, seq))
    return jax.shard_map(
        per_device, mesh=grid, in_specs=in_specs, out_specs=out_specs, check_vma=False
    )
```

```python
import functools

import jax
import jax.numpy as jnp
from jax import lax
from jax.experimental import pallas as pl
from jax.experimental.pallas import tpu as pltpu
from jax.sharding import Mesh, PartitionSpec as P

STATE = 16
RANK = 128


def gather_a2a(block, axis, dim):
    count = lax.axis_size(axis)
    copies = jnp.broadcast_to(block[None], (count,) + block.shape)
    stacked = lax.all_to_all(copies, axis, split_axis=0, concat_axis=0, tiled=True)
    moved = jnp.moveaxis(stacked, 0, dim)
    shape = list(block.shape)
    shape[dim] = shape[dim] * count
    return moved.reshape(shape)


LANES = 128
SUB = 8


def scan_body(emit, into_ref, outof_ref, rate_ref, value_ref, decay_ref, start_ref, skip_ref, *outs):
    steps = rate_ref.shape[0]
    states = decay_ref.shape[0]
    decay = [decay_ref[n] for n in range(states)]
    if emit:
        out_ref, = outs
        skip = skip_ref[...]
    else:
        end_ref, total_ref = outs

    def step(t, carry):
        held, acc = carry
        rate = rate_ref[t]
        value = value_ref[t]
        push = rate * value
        row = t * states
        new = []
        result = skip * value if emit else None
        for n in range(states):
            s = jnp.exp(rate * decay[n]) * held[n] + push * into_ref[row + n]
            if emit:
                result = result + outof_ref[row + n] * s
            new.append(s)
        if emit:
            out_ref[t] = result
        else:
            acc = acc + rate
        return (tuple(new), acc)

    held0 = tuple(start_ref[n] for n in range(states))
    acc0 = jnp.zeros((SUB, LANES), jnp.float32)
    held, acc = lax.fori_loop(0, steps, step, (held0, acc0), unroll=2)
    if not emit:
        for n in range(states):
            end_ref[n] = held[n]
        total_ref[0] = acc


def run_scan(emit, into, outof, rate, value, decay, start, skip):
    steps, rows, lanes = rate.shape
    states = decay.shape[0]
    chunks = rows // SUB
    smem = pl.BlockSpec(memory_space=pltpu.MemorySpace.SMEM)
    seq_spec = pl.BlockSpec((steps, SUB, lanes), lambda i: (0, i, 0))
    st_spec = pl.BlockSpec((states, SUB, lanes), lambda i: (0, i, 0))
    skip_spec = pl.BlockSpec((SUB, lanes), lambda i: (i, 0))
    if emit:
        out_shape = jax.ShapeDtypeStruct((steps, rows, lanes), jnp.float32)
        out_specs = seq_spec
    else:
        out_shape = (
            jax.ShapeDtypeStruct((states, rows, lanes), jnp.float32),
            jax.ShapeDtypeStruct((1, rows, lanes), jnp.float32),
        )
        out_specs = (st_spec, pl.BlockSpec((1, SUB, lanes), lambda i: (0, i, 0)))
    flops = steps * rows * lanes * states * 6
    return pl.pallas_call(
        functools.partial(scan_body, emit),
        grid=(chunks,),
        in_specs=[smem, smem, seq_spec, seq_spec, st_spec, st_spec, skip_spec],
        out_specs=out_specs,
        out_shape=out_shape,
        cost_estimate=pl.CostEstimate(
            flops=flops,
            transcendentals=steps * rows * lanes * states,
            bytes_accessed=(3 if emit else 2) * steps * rows * lanes * 4,
        ),
    )(into, outof, rate, value, decay, start, skip)


def per_device(
    hidden,
    lengths,
    slot_request,
    norm_gain,
    in_weight,
    conv_weight,
    conv_bias,
    xproj_weight,
    dt_weight,
    dt_bias,
    a_log,
    skip_gain,
    out_weight,
):
    seq = ("sz", "sy")
    rows_n = lax.axis_size("sz")
    cols_n = lax.axis_size("sy")
    seq_count = rows_n * cols_n
    seq_index = lax.axis_index(seq)
    req_index = lax.axis_index("req")
    rows = hidden.shape[1]
    span = rows * seq_count
    width = in_weight.shape[2]
    taps_count = conv_weight.shape[0]
    state_count = a_log.shape[0]
    total_inner = a_log.shape[1]
    model = hidden.shape[2]
    tokens = hidden[0].astype(jnp.float32)
    scale = lax.rsqrt(jnp.mean(tokens * tokens, axis=-1, keepdims=True) + 1e-05)
    normed = (tokens * scale * norm_gain.astype(jnp.float32)).astype(jnp.bfloat16)
    normed_all = lax.all_gather(normed, seq, axis=0, tiled=True)
    w_in = gather_a2a(in_weight, "req", 1)
    xproj_w, dt_w, dt_b, _ = lax.optimization_barrier((xproj_weight, dt_weight, dt_bias, normed))
    xproj_full = gather_a2a(xproj_w, seq, 0)
    dt_full = gather_a2a(dt_w, seq, 1)
    dt_bias_full = gather_a2a(dt_b, seq, 0)
    w_in, xproj_full, dt_full, dt_bias_full = lax.optimization_barrier(
        (w_in, xproj_full, dt_full, dt_bias_full)
    )
    w_late, _ = lax.optimization_barrier((out_weight, normed_all))
    w_col = lax.all_gather(gather_a2a(w_late, "req", 1), "sz", axis=0, tiled=False)
    w_flat = jnp.concatenate((w_in[0], w_in[1]), axis=1)
    both = jnp.dot(normed_all, w_flat, preferred_element_type=jnp.float32)
    xin = both[:, :width]
    zgate = both[:, width:].astype(jnp.bfloat16)
    z_grid = lax.all_to_all(
        zgate.reshape(rows_n, span // rows_n, width), "sz", split_axis=0, concat_axis=0, tiled=True
    )
    padded = jnp.pad(xin, ((taps_count - 1, 0), (0, 0)))
    taps = conv_weight.astype(jnp.float32)
    convolved = conv_bias.astype(jnp.float32) + jnp.zeros_like(xin)
    for tap in range(taps_count):
        convolved = convolved + taps[tap] * padded[tap : tap + span, :]
    inner = jax.nn.silu(convolved).astype(jnp.bfloat16)
    inner_tok = lax.all_to_all(inner, seq, split_axis=0, concat_axis=1, tiled=True)
    proj = jnp.dot(inner_tok, xproj_full, preferred_element_type=jnp.float32)
    length_here = lax.dynamic_index_in_dim(lengths, req_index, 0, keepdims=False)
    positions = seq_index * rows + jnp.arange(rows, dtype=jnp.int32)
    live = (positions < length_here).astype(jnp.float32)
    rate_low = proj[:, :RANK].astype(jnp.bfloat16)
    delta_tok = (
        jax.nn.softplus(
            jnp.dot(rate_low, dt_full, preferred_element_type=jnp.float32)
            + dt_bias_full.astype(jnp.float32)
        )
        * live[:, None]
    )
    decay = -jnp.exp(a_log)
    lanes = 128
    groups = total_inner // lanes
    inner_f = inner_tok.astype(jnp.float32)
    into = proj[:, RANK : RANK + STATE].reshape(-1)
    outof = proj[:, RANK + STATE :].reshape(-1)
    rate_l = delta_tok.reshape(rows, groups, lanes)
    value_l = inner_f.reshape(rows, groups, lanes)
    decay_l = decay.reshape(state_count, groups, lanes)
    skip_l = skip_gain.reshape(groups, lanes)
    end_l, total_l = run_scan(
        False, into, outof, rate_l, value_l, decay_l,
        jnp.zeros((state_count, groups, lanes), jnp.float32), skip_l,
    )
    pair = jnp.concatenate(
        (end_l.reshape(state_count, total_inner), total_l.reshape(1, total_inner))
    ).reshape(state_count + 1, seq_count, width)
    pair_ch = lax.all_to_all(pair, seq, split_axis=1, concat_axis=1, tiled=True)
    decay_ch = lax.dynamic_slice_in_dim(decay, seq_index * width, width, 1)
    falls = jnp.exp(pair_ch[state_count][None] * decay_ch[:, None, :])
    carry = jnp.zeros((state_count, width), jnp.float32)
    carries = []
    for block in range(seq_count):
        carries.append(carry)
        carry = falls[:, block] * carry + pair_ch[:state_count, block]
    carry_ch = jnp.stack(carries, axis=1)
    carry_in = lax.all_to_all(carry_ch, seq, split_axis=1, concat_axis=1, tiled=True)
    out_l = run_scan(
        True, into, outof, rate_l, value_l, decay_l,
        carry_in.reshape(state_count, groups, lanes), skip_l,
    )
    scanned = out_l.reshape(rows, rows_n, cols_n, width).astype(jnp.bfloat16)
    scanned_grid = lax.all_to_all(scanned, "sy", split_axis=2, concat_axis=0, tiled=True)
    z_here = z_grid.reshape(rows_n, cols_n, rows, width).transpose(1, 2, 0, 3)
    gated = (
        scanned_grid.reshape(cols_n, rows, rows_n, width).astype(jnp.float32)
        * jax.nn.silu(z_here.astype(jnp.float32))
    ).astype(jnp.bfloat16)
    partial = jnp.einsum(
        "ktac,acd->ktd", gated, w_col, preferred_element_type=jnp.float32
    ).astype(jnp.bfloat16)
    branch = lax.psum_scatter(
        partial.reshape(cols_n * rows, model), "sy", scatter_dimension=0, tiled=True
    ).astype(jnp.float32)
    slot_all = gather_a2a(carry[None], "req", 0)
    picked = (slot_request == req_index).astype(jnp.float32)
    final_state = jnp.sum(picked[:, None, None] * slot_all, axis=0, keepdims=True)
    mixed = (tokens + branch).astype(jnp.bfloat16)[None]
    return (mixed, final_state)


def solution(mesh):
    seq_n = mesh.shape["seq"]
    rows_n = 1
    while rows_n * rows_n < seq_n:
        rows_n *= 2
    grid = Mesh(mesh.devices.reshape(mesh.shape["req"], rows_n, seq_n // rows_n), ("req", "sz", "sy"))
    seq = ("sz", "sy")
    in_specs = (
        P("req", seq, None),
        P(),
        P(),
        P(),
        P(None, "req", seq),
        P(None, seq),
        P(seq),
        P(seq, None),
        P(None, seq),
        P(seq),
        P(),
        P(),
        P(seq, "req"),
    )
    out_specs = (P("req", seq, None), P("req", None, seq))
    return jax.shard_map(
        per_device, mesh=grid, in_specs=in_specs, out_specs=out_specs, check_vma=False
    )
```

```python
import functools

import jax
import jax.numpy as jnp
from jax import lax
from jax.experimental import pallas as pl
from jax.experimental.pallas import tpu as pltpu
from jax.sharding import Mesh, PartitionSpec as P

STATE = 16
RANK = 128


def gather_a2a(block, axis, dim):
    count = lax.axis_size(axis)
    copies = jnp.broadcast_to(block[None], (count,) + block.shape)
    stacked = lax.all_to_all(copies, axis, split_axis=0, concat_axis=0, tiled=True)
    moved = jnp.moveaxis(stacked, 0, dim)
    shape = list(block.shape)
    shape[dim] = shape[dim] * count
    return moved.reshape(shape)


LANES = 128
SUB = 8


def scan_body(emit, into_ref, outof_ref, rate_ref, value_ref, decay_ref, start_ref, skip_ref, *outs):
    steps = rate_ref.shape[0]
    states = decay_ref.shape[0]
    decay = [decay_ref[n] for n in range(states)]
    if emit:
        out_ref, = outs
        skip = skip_ref[...]
    else:
        end_ref, total_ref = outs

    def step(t, carry):
        held, acc = carry
        rate = rate_ref[t]
        value = value_ref[t]
        push = rate * value
        row = t * states
        new = []
        result = skip * value if emit else None
        for n in range(states):
            s = jnp.exp(rate * decay[n]) * held[n] + push * into_ref[row + n]
            if emit:
                result = result + outof_ref[row + n] * s
            new.append(s)
        if emit:
            out_ref[t] = result
        else:
            acc = acc + rate
        return (tuple(new), acc)

    held0 = tuple(start_ref[n] for n in range(states))
    acc0 = jnp.zeros((SUB, LANES), jnp.float32)
    held, acc = lax.fori_loop(0, steps, step, (held0, acc0), unroll=2)
    if not emit:
        for n in range(states):
            end_ref[n] = held[n]
        total_ref[0] = acc


def run_scan(emit, into, outof, rate, value, decay, start, skip):
    steps, rows, lanes = rate.shape
    states = decay.shape[0]
    chunks = rows // SUB
    smem = pl.BlockSpec(memory_space=pltpu.MemorySpace.SMEM)
    seq_spec = pl.BlockSpec((steps, SUB, lanes), lambda i: (0, i, 0))
    st_spec = pl.BlockSpec((states, SUB, lanes), lambda i: (0, i, 0))
    skip_spec = pl.BlockSpec((SUB, lanes), lambda i: (i, 0))
    if emit:
        out_shape = jax.ShapeDtypeStruct((steps, rows, lanes), jnp.float32)
        out_specs = seq_spec
    else:
        out_shape = (
            jax.ShapeDtypeStruct((states, rows, lanes), jnp.float32),
            jax.ShapeDtypeStruct((1, rows, lanes), jnp.float32),
        )
        out_specs = (st_spec, pl.BlockSpec((1, SUB, lanes), lambda i: (0, i, 0)))
    flops = steps * rows * lanes * states * 6
    return pl.pallas_call(
        functools.partial(scan_body, emit),
        grid=(chunks,),
        in_specs=[smem, smem, seq_spec, seq_spec, st_spec, st_spec, skip_spec],
        out_specs=out_specs,
        out_shape=out_shape,
        cost_estimate=pl.CostEstimate(
            flops=flops,
            transcendentals=steps * rows * lanes * states,
            bytes_accessed=(3 if emit else 2) * steps * rows * lanes * 4,
        ),
    )(into, outof, rate, value, decay, start, skip)


def combine_body(pair_ref, decay_ref, carries_ref, final_ref):
    blocks = pair_ref.shape[0]
    states = decay_ref.shape[0]
    decay = decay_ref[...]
    carry = jnp.zeros(decay.shape, jnp.float32)
    for block in range(blocks):
        carries_ref[block] = carry
        rows = pair_ref[block]
        carry = jnp.exp(rows[states : states + 1] * decay) * carry + rows[:states]
    final_ref[...] = carry


def run_combine(pair, decay):
    blocks = pair.shape[0]
    states, width = decay.shape
    vmem = pl.BlockSpec(memory_space=pltpu.MemorySpace.VMEM)
    return pl.pallas_call(
        combine_body,
        in_specs=[vmem, vmem],
        out_specs=(vmem, vmem),
        out_shape=(
            jax.ShapeDtypeStruct((blocks, states, width), jnp.float32),
            jax.ShapeDtypeStruct((states, width), jnp.float32),
        ),
    )(pair, decay)


def per_device(
    hidden,
    lengths,
    slot_request,
    norm_gain,
    in_weight,
    conv_weight,
    conv_bias,
    xproj_weight,
    dt_weight,
    dt_bias,
    a_log,
    skip_gain,
    out_weight,
):
    seq = ("sz", "sy")
    rows_n = lax.axis_size("sz")
    cols_n = lax.axis_size("sy")
    seq_count = rows_n * cols_n
    seq_index = lax.axis_index(seq)
    req_index = lax.axis_index("req")
    rows = hidden.shape[1]
    span = rows * seq_count
    width = in_weight.shape[2]
    taps_count = conv_weight.shape[0]
    state_count = a_log.shape[0]
    total_inner = a_log.shape[1]
    model = hidden.shape[2]
    tokens = hidden[0].astype(jnp.float32)
    scale = lax.rsqrt(jnp.mean(tokens * tokens, axis=-1, keepdims=True) + 1e-05)
    normed = (tokens * scale * norm_gain.astype(jnp.float32)).astype(jnp.bfloat16)
    normed_all = lax.all_gather(normed, seq, axis=0, tiled=True)
    w_in = gather_a2a(in_weight, "req", 1)
    xproj_w, dt_w, dt_b, _ = lax.optimization_barrier((xproj_weight, dt_weight, dt_bias, normed))
    proj_cols = xproj_w.shape[1]
    small = jnp.concatenate((xproj_w, dt_w.T, dt_b[:, None]), axis=1)
    small_full = gather_a2a(small, seq, 0)
    xproj_full = small_full[:, :proj_cols]
    dt_full = small_full[:, proj_cols : proj_cols + RANK].T
    dt_bias_full = small_full[:, proj_cols + RANK]
    w_in, xproj_full, dt_full, dt_bias_full = lax.optimization_barrier(
        (w_in, xproj_full, dt_full, dt_bias_full)
    )
    w_late, _ = lax.optimization_barrier((out_weight, normed_all))
    w_col = lax.all_gather(gather_a2a(w_late, "req", 1), "sz", axis=0, tiled=False)
    w_flat = jnp.concatenate((w_in[0], w_in[1]), axis=1)
    both = jnp.dot(normed_all, w_flat, preferred_element_type=jnp.float32)
    xin = both[:, :width]
    zgate = both[:, width:].astype(jnp.bfloat16)
    z_grid = lax.all_to_all(
        zgate.reshape(rows_n, span // rows_n, width), "sz", split_axis=0, concat_axis=0, tiled=True
    )
    padded = jnp.pad(xin, ((taps_count - 1, 0), (0, 0)))
    taps = conv_weight.astype(jnp.float32)
    convolved = conv_bias.astype(jnp.float32) + jnp.zeros_like(xin)
    for tap in range(taps_count):
        convolved = convolved + taps[tap] * padded[tap : tap + span, :]
    inner = jax.nn.silu(convolved).astype(jnp.bfloat16)
    inner_tok = lax.all_to_all(inner, seq, split_axis=0, concat_axis=1, tiled=True)
    proj = jnp.dot(inner_tok, xproj_full, preferred_element_type=jnp.float32)
    length_here = lax.dynamic_index_in_dim(lengths, req_index, 0, keepdims=False)
    positions = seq_index * rows + jnp.arange(rows, dtype=jnp.int32)
    live = (positions < length_here).astype(jnp.float32)
    rate_low = proj[:, :RANK].astype(jnp.bfloat16)
    delta_tok = (
        jax.nn.softplus(
            jnp.dot(rate_low, dt_full, preferred_element_type=jnp.float32)
            + dt_bias_full.astype(jnp.float32)
        )
        * live[:, None]
    )
    decay = -jnp.exp(a_log)
    lanes = 128
    groups = total_inner // lanes
    inner_f = inner_tok.astype(jnp.float32)
    into = proj[:, RANK : RANK + STATE].reshape(-1)
    outof = proj[:, RANK + STATE :].reshape(-1)
    rate_l = delta_tok.reshape(rows, groups, lanes)
    value_l = inner_f.reshape(rows, groups, lanes)
    decay_l = decay.reshape(state_count, groups, lanes)
    skip_l = skip_gain.reshape(groups, lanes)
    end_l, total_l = run_scan(
        False, into, outof, rate_l, value_l, decay_l,
        jnp.zeros((state_count, groups, lanes), jnp.float32), skip_l,
    )
    pair = jnp.concatenate(
        (end_l.reshape(state_count, total_inner), total_l.reshape(1, total_inner))
    ).reshape(state_count + 1, seq_count, width)
    pair_ch = lax.all_to_all(
        jnp.swapaxes(pair, 0, 1), seq, split_axis=0, concat_axis=0, tiled=True
    )
    decay_ch = lax.dynamic_slice_in_dim(decay, seq_index * width, width, 1)
    carry_ch, carry = run_combine(pair_ch, decay_ch)
    carry_in = lax.all_to_all(carry_ch, seq, split_axis=0, concat_axis=0, tiled=True)
    carry_in = jnp.swapaxes(carry_in, 0, 1).reshape(state_count, total_inner)
    out_l = run_scan(
        True, into, outof, rate_l, value_l, decay_l,
        carry_in.reshape(state_count, groups, lanes), skip_l,
    )
    scanned = out_l.reshape(rows, rows_n, cols_n, width).astype(jnp.bfloat16)
    scanned_grid = lax.all_to_all(scanned, "sy", split_axis=2, concat_axis=0, tiled=True)
    z_here = z_grid.reshape(rows_n, cols_n, rows, width).transpose(1, 2, 0, 3)
    gated = (
        scanned_grid.reshape(cols_n, rows, rows_n, width).astype(jnp.float32)
        * jax.nn.silu(z_here.astype(jnp.float32))
    ).astype(jnp.bfloat16)
    partial = jnp.einsum(
        "ktac,acd->ktd", gated, w_col, preferred_element_type=jnp.float32
    ).astype(jnp.bfloat16)
    branch = lax.psum_scatter(
        partial.reshape(cols_n * rows, model), "sy", scatter_dimension=0, tiled=True
    ).astype(jnp.float32)
    slot_all = gather_a2a(carry[None], "req", 0)
    picked = (slot_request == req_index).astype(jnp.float32)
    final_state = jnp.sum(picked[:, None, None] * slot_all, axis=0, keepdims=True)
    mixed = (tokens + branch).astype(jnp.bfloat16)[None]
    return (mixed, final_state)


def solution(mesh):
    seq_n = mesh.shape["seq"]
    rows_n = 1
    while rows_n * rows_n < seq_n:
        rows_n *= 2
    grid = Mesh(mesh.devices.reshape(mesh.shape["req"], rows_n, seq_n // rows_n), ("req", "sz", "sy"))
    seq = ("sz", "sy")
    in_specs = (
        P("req", seq, None),
        P(),
        P(),
        P(),
        P(None, "req", seq),
        P(None, seq),
        P(seq),
        P(seq, None),
        P(None, seq),
        P(seq),
        P(),
        P(),
        P(seq, "req"),
    )
    out_specs = (P("req", seq, None), P("req", None, seq))
    return jax.shard_map(
        per_device, mesh=grid, in_specs=in_specs, out_specs=out_specs, check_vma=False
    )
```

```python
import functools

import jax
import jax.numpy as jnp
from jax import lax
from jax.experimental import pallas as pl
from jax.experimental.pallas import tpu as pltpu
from jax.sharding import Mesh, PartitionSpec as P

STATE = 16
RANK = 128


def gather_a2a(block, axis, dim):
    count = lax.axis_size(axis)
    copies = jnp.broadcast_to(block[None], (count,) + block.shape)
    stacked = lax.all_to_all(copies, axis, split_axis=0, concat_axis=0, tiled=True)
    moved = jnp.moveaxis(stacked, 0, dim)
    shape = list(block.shape)
    shape[dim] = shape[dim] * count
    return moved.reshape(shape)


LANES = 128
SUB = 8


def scan_body(emit, into_ref, outof_ref, rate_ref, value_ref, decay_ref, start_ref, skip_ref, *outs):
    steps = rate_ref.shape[0]
    states = decay_ref.shape[0]
    decay = [decay_ref[n] for n in range(states)]
    if emit:
        out_ref, = outs
        skip = skip_ref[...]
    else:
        end_ref, total_ref = outs

    def step(t, carry):
        held, acc = carry
        rate = rate_ref[t]
        value = value_ref[t]
        push = rate * value
        row = t * states
        new = []
        result = skip * value if emit else None
        for n in range(states):
            s = jnp.exp(rate * decay[n]) * held[n] + push * into_ref[row + n]
            if emit:
                result = result + outof_ref[row + n] * s
            new.append(s)
        if emit:
            out_ref[t] = result
        else:
            acc = acc + rate
        return (tuple(new), acc)

    held0 = tuple(start_ref[n] for n in range(states))
    acc0 = jnp.zeros((SUB, LANES), jnp.float32)
    held, acc = lax.fori_loop(0, steps, step, (held0, acc0), unroll=2)
    if not emit:
        for n in range(states):
            end_ref[n] = held[n]
        total_ref[0] = acc


def run_scan(emit, into, outof, rate, value, decay, start, skip):
    steps, rows, lanes = rate.shape
    states = decay.shape[0]
    chunks = rows // SUB
    smem = pl.BlockSpec(memory_space=pltpu.MemorySpace.SMEM)
    seq_spec = pl.BlockSpec((steps, SUB, lanes), lambda i: (0, i, 0))
    st_spec = pl.BlockSpec((states, SUB, lanes), lambda i: (0, i, 0))
    skip_spec = pl.BlockSpec((SUB, lanes), lambda i: (i, 0))
    if emit:
        out_shape = jax.ShapeDtypeStruct((steps, rows, lanes), jnp.float32)
        out_specs = seq_spec
    else:
        out_shape = (
            jax.ShapeDtypeStruct((states, rows, lanes), jnp.float32),
            jax.ShapeDtypeStruct((1, rows, lanes), jnp.float32),
        )
        out_specs = (st_spec, pl.BlockSpec((1, SUB, lanes), lambda i: (0, i, 0)))
    flops = steps * rows * lanes * states * 6
    return pl.pallas_call(
        functools.partial(scan_body, emit),
        grid=(chunks,),
        in_specs=[smem, smem, seq_spec, seq_spec, st_spec, st_spec, skip_spec],
        out_specs=out_specs,
        out_shape=out_shape,
        cost_estimate=pl.CostEstimate(
            flops=flops,
            transcendentals=steps * rows * lanes * states,
            bytes_accessed=(3 if emit else 2) * steps * rows * lanes * 4,
        ),
    )(into, outof, rate, value, decay, start, skip)


def combine_body(pair_ref, decay_ref, carries_ref, final_ref):
    blocks = pair_ref.shape[0]
    states = decay_ref.shape[0]
    decay = decay_ref[...]
    carry = jnp.zeros(decay.shape, jnp.float32)
    for block in range(blocks):
        carries_ref[block] = carry
        rows = pair_ref[block]
        carry = jnp.exp(rows[states : states + 1] * decay) * carry + rows[:states]
    final_ref[...] = carry


def run_combine(pair, decay):
    blocks = pair.shape[0]
    states, width = decay.shape
    vmem = pl.BlockSpec(memory_space=pltpu.MemorySpace.VMEM)
    return pl.pallas_call(
        combine_body,
        in_specs=[vmem, vmem],
        out_specs=(vmem, vmem),
        out_shape=(
            jax.ShapeDtypeStruct((blocks, states, width), jnp.float32),
            jax.ShapeDtypeStruct((states, width), jnp.float32),
        ),
    )(pair, decay)


def per_device(
    hidden,
    lengths,
    slot_request,
    norm_gain,
    in_weight,
    conv_weight,
    conv_bias,
    xproj_weight,
    dt_weight,
    dt_bias,
    a_log,
    skip_gain,
    out_weight,
):
    seq = ("sz", "sy")
    rows_n = lax.axis_size("sz")
    cols_n = lax.axis_size("sy")
    seq_count = rows_n * cols_n
    seq_index = lax.axis_index(seq)
    req_index = lax.axis_index("req")
    rows = hidden.shape[1]
    span = rows * seq_count
    width = in_weight.shape[2]
    taps_count = conv_weight.shape[0]
    state_count = a_log.shape[0]
    total_inner = a_log.shape[1]
    model = hidden.shape[2]
    tokens = hidden[0].astype(jnp.float32)
    scale = lax.rsqrt(jnp.mean(tokens * tokens, axis=-1, keepdims=True) + 1e-05)
    normed = (tokens * scale * norm_gain.astype(jnp.float32)).astype(jnp.bfloat16)
    normed_all = lax.all_gather(normed, seq, axis=0, tiled=True)
    pieces = jnp.concatenate((in_weight, out_weight.T[None]), axis=0)
    pieces_all = gather_a2a(pieces, "req", 1)
    w_in = pieces_all[:2]
    w_out_t = pieces_all[2]
    xproj_w, dt_w, dt_b, _ = lax.optimization_barrier((xproj_weight, dt_weight, dt_bias, normed))
    proj_cols = xproj_w.shape[1]
    small = jnp.concatenate((xproj_w.T, dt_w, dt_b[None]), axis=0)
    copies = jnp.broadcast_to(small[None], (seq_count,) + small.shape)
    small_all = lax.all_to_all(copies, seq, split_axis=0, concat_axis=0, tiled=True)
    xproj_full = jnp.swapaxes(small_all[:, :proj_cols], 1, 2).reshape(total_inner, proj_cols)
    dt_full = jnp.swapaxes(small_all[:, proj_cols : proj_cols + RANK], 0, 1).reshape(
        RANK, total_inner
    )
    dt_bias_full = small_all[:, proj_cols + RANK].reshape(total_inner)
    w_in, xproj_full, dt_full, dt_bias_full = lax.optimization_barrier(
        (w_in, xproj_full, dt_full, dt_bias_full)
    )
    w_flat = jnp.concatenate((w_in[0], w_in[1]), axis=1)
    both = jnp.dot(normed_all, w_flat, preferred_element_type=jnp.float32)
    w_late, _ = lax.optimization_barrier((w_out_t, normed_all))
    w_col = lax.all_gather(w_late.T, "sz", axis=0, tiled=False)
    xin = both[:, :width]
    zgate = both[:, width:].astype(jnp.bfloat16)
    z_grid = lax.all_to_all(
        zgate.reshape(rows_n, span // rows_n, width), "sz", split_axis=0, concat_axis=0, tiled=True
    )
    padded = jnp.pad(xin, ((taps_count - 1, 0), (0, 0)))
    taps = conv_weight.astype(jnp.float32)
    convolved = conv_bias.astype(jnp.float32) + jnp.zeros_like(xin)
    for tap in range(taps_count):
        convolved = convolved + taps[tap] * padded[tap : tap + span, :]
    inner = jax.nn.silu(convolved).astype(jnp.bfloat16)
    inner_tok = lax.all_to_all(inner, seq, split_axis=0, concat_axis=1, tiled=True)
    proj = jnp.dot(inner_tok, xproj_full, preferred_element_type=jnp.float32)
    length_here = lax.dynamic_index_in_dim(lengths, req_index, 0, keepdims=False)
    positions = seq_index * rows + jnp.arange(rows, dtype=jnp.int32)
    live = (positions < length_here).astype(jnp.float32)
    rate_low = proj[:, :RANK].astype(jnp.bfloat16)
    delta_tok = (
        jax.nn.softplus(
            jnp.dot(rate_low, dt_full, preferred_element_type=jnp.float32)
            + dt_bias_full.astype(jnp.float32)
        )
        * live[:, None]
    )
    decay = -jnp.exp(a_log)
    lanes = 128
    groups = total_inner // lanes
    inner_f = inner_tok.astype(jnp.float32)
    into = proj[:, RANK : RANK + STATE].reshape(-1)
    outof = proj[:, RANK + STATE :].reshape(-1)
    rate_l = delta_tok.reshape(rows, groups, lanes)
    value_l = inner_f.reshape(rows, groups, lanes)
    decay_l = decay.reshape(state_count, groups, lanes)
    skip_l = skip_gain.reshape(groups, lanes)
    end_l, total_l = run_scan(
        False, into, outof, rate_l, value_l, decay_l,
        jnp.zeros((state_count, groups, lanes), jnp.float32), skip_l,
    )
    pair = jnp.concatenate(
        (end_l.reshape(state_count, total_inner), total_l.reshape(1, total_inner))
    ).reshape(state_count + 1, seq_count, width)
    pair_ch = lax.all_to_all(
        jnp.swapaxes(pair, 0, 1), seq, split_axis=0, concat_axis=0, tiled=True
    )
    decay_ch = lax.dynamic_slice_in_dim(decay, seq_index * width, width, 1)
    carry_ch, carry = run_combine(pair_ch, decay_ch)
    carry_in = lax.all_to_all(carry_ch, seq, split_axis=0, concat_axis=0, tiled=True)
    carry_in = jnp.swapaxes(carry_in, 0, 1).reshape(state_count, total_inner)
    out_l = run_scan(
        True, into, outof, rate_l, value_l, decay_l,
        carry_in.reshape(state_count, groups, lanes), skip_l,
    )
    scanned = out_l.reshape(rows, rows_n, cols_n, width).astype(jnp.bfloat16)
    scanned_grid = lax.all_to_all(scanned, "sy", split_axis=2, concat_axis=0, tiled=True)
    z_here = z_grid.reshape(rows_n, cols_n, rows, width).transpose(1, 2, 0, 3)
    gated = (
        scanned_grid.reshape(cols_n, rows, rows_n, width).astype(jnp.float32)
        * jax.nn.silu(z_here.astype(jnp.float32))
    ).astype(jnp.bfloat16)
    partial = jnp.einsum(
        "ktac,acd->ktd", gated, w_col, preferred_element_type=jnp.float32
    ).astype(jnp.bfloat16)
    branch = lax.psum_scatter(
        partial.reshape(cols_n * rows, model), "sy", scatter_dimension=0, tiled=True
    ).astype(jnp.float32)
    slot_all = gather_a2a(carry[None], "req", 0)
    picked = (slot_request == req_index).astype(jnp.float32)
    final_state = jnp.sum(picked[:, None, None] * slot_all, axis=0, keepdims=True)
    mixed = (tokens + branch).astype(jnp.bfloat16)[None]
    return (mixed, final_state)


def solution(mesh):
    seq_n = mesh.shape["seq"]
    rows_n = 1
    while rows_n * rows_n < seq_n:
        rows_n *= 2
    grid = Mesh(mesh.devices.reshape(mesh.shape["req"], rows_n, seq_n // rows_n), ("req", "sz", "sy"))
    seq = ("sz", "sy")
    in_specs = (
        P("req", seq, None),
        P(),
        P(),
        P(),
        P(None, "req", seq),
        P(None, seq),
        P(seq),
        P(seq, None),
        P(None, seq),
        P(seq),
        P(),
        P(),
        P(seq, "req"),
    )
    out_specs = (P("req", seq, None), P("req", None, seq))
    return jax.shard_map(
        per_device, mesh=grid, in_specs=in_specs, out_specs=out_specs, check_vma=False
    )
```

```python
import functools

import jax
import jax.numpy as jnp
from jax import lax
from jax.experimental import pallas as pl
from jax.experimental.pallas import tpu as pltpu
from jax.sharding import Mesh, PartitionSpec as P

STATE = 16
RANK = 128


def gather_a2a(block, axis, dim):
    count = lax.axis_size(axis)
    copies = jnp.broadcast_to(block[None], (count,) + block.shape)
    stacked = lax.all_to_all(copies, axis, split_axis=0, concat_axis=0, tiled=True)
    moved = jnp.moveaxis(stacked, 0, dim)
    shape = list(block.shape)
    shape[dim] = shape[dim] * count
    return moved.reshape(shape)


LANES = 128
SUB = 8


def scan_body(emit, into_ref, outof_ref, rate_ref, value_ref, decay_ref, start_ref, skip_ref, *outs):
    steps = rate_ref.shape[0]
    states = decay_ref.shape[0]
    decay = [decay_ref[n] for n in range(states)]
    if emit:
        out_ref, = outs
        skip = skip_ref[...]
    else:
        end_ref, total_ref = outs

    def step(t, carry):
        held, acc = carry
        rate = rate_ref[t]
        value = value_ref[t]
        push = rate * value
        row = t * states
        new = []
        result = skip * value if emit else None
        for n in range(states):
            s = jnp.exp(rate * decay[n]) * held[n] + push * into_ref[row + n]
            if emit:
                result = result + outof_ref[row + n] * s
            new.append(s)
        if emit:
            out_ref[t] = result
        else:
            acc = acc + rate
        return (tuple(new), acc)

    held0 = tuple(start_ref[n] for n in range(states))
    acc0 = jnp.zeros((SUB, LANES), jnp.float32)
    held, acc = lax.fori_loop(0, steps, step, (held0, acc0), unroll=4)
    if not emit:
        for n in range(states):
            end_ref[n] = held[n]
        total_ref[0] = acc


def run_scan(emit, into, outof, rate, value, decay, start, skip):
    steps, rows, lanes = rate.shape
    states = decay.shape[0]
    chunks = rows // SUB
    smem = pl.BlockSpec(memory_space=pltpu.MemorySpace.SMEM)
    seq_spec = pl.BlockSpec((steps, SUB, lanes), lambda i: (0, i, 0))
    st_spec = pl.BlockSpec((states, SUB, lanes), lambda i: (0, i, 0))
    skip_spec = pl.BlockSpec((SUB, lanes), lambda i: (i, 0))
    if emit:
        out_shape = jax.ShapeDtypeStruct((steps, rows, lanes), jnp.float32)
        out_specs = seq_spec
    else:
        out_shape = (
            jax.ShapeDtypeStruct((states, rows, lanes), jnp.float32),
            jax.ShapeDtypeStruct((1, rows, lanes), jnp.float32),
        )
        out_specs = (st_spec, pl.BlockSpec((1, SUB, lanes), lambda i: (0, i, 0)))
    flops = steps * rows * lanes * states * 6
    return pl.pallas_call(
        functools.partial(scan_body, emit),
        grid=(chunks,),
        in_specs=[smem, smem, seq_spec, seq_spec, st_spec, st_spec, skip_spec],
        out_specs=out_specs,
        out_shape=out_shape,
        cost_estimate=pl.CostEstimate(
            flops=flops,
            transcendentals=steps * rows * lanes * states,
            bytes_accessed=(3 if emit else 2) * steps * rows * lanes * 4,
        ),
    )(into, outof, rate, value, decay, start, skip)


def combine_body(pair_ref, decay_ref, carries_ref, final_ref):
    blocks = pair_ref.shape[0]
    states = decay_ref.shape[0]
    decay = decay_ref[...]
    carry = jnp.zeros(decay.shape, jnp.float32)
    for block in range(blocks):
        carries_ref[block] = carry
        rows = pair_ref[block]
        carry = jnp.exp(rows[states : states + 1] * decay) * carry + rows[:states]
    final_ref[...] = carry


def run_combine(pair, decay):
    blocks = pair.shape[0]
    states, width = decay.shape
    vmem = pl.BlockSpec(memory_space=pltpu.MemorySpace.VMEM)
    return pl.pallas_call(
        combine_body,
        in_specs=[vmem, vmem],
        out_specs=(vmem, vmem),
        out_shape=(
            jax.ShapeDtypeStruct((blocks, states, width), jnp.float32),
            jax.ShapeDtypeStruct((states, width), jnp.float32),
        ),
    )(pair, decay)


def per_device(
    hidden,
    lengths,
    slot_request,
    norm_gain,
    in_weight,
    conv_weight,
    conv_bias,
    xproj_weight,
    dt_weight,
    dt_bias,
    a_log,
    skip_gain,
    out_weight,
):
    seq = ("sz", "sy")
    rows_n = lax.axis_size("sz")
    cols_n = lax.axis_size("sy")
    seq_count = rows_n * cols_n
    seq_index = lax.axis_index(seq)
    req_index = lax.axis_index("req")
    rows = hidden.shape[1]
    span = rows * seq_count
    width = in_weight.shape[2]
    taps_count = conv_weight.shape[0]
    state_count = a_log.shape[0]
    total_inner = a_log.shape[1]
    model = hidden.shape[2]
    tokens = hidden[0].astype(jnp.float32)
    scale = lax.rsqrt(jnp.mean(tokens * tokens, axis=-1, keepdims=True) + 1e-05)
    normed = (tokens * scale * norm_gain.astype(jnp.float32)).astype(jnp.bfloat16)
    normed_all = lax.all_gather(normed, seq, axis=0, tiled=True)
    pieces = jnp.concatenate((in_weight[0], in_weight[1], out_weight.T), axis=1)
    pieces_all = gather_a2a(pieces, "req", 0)
    w_flat = pieces_all[:, : 2 * width]
    w_out_t = pieces_all[:, 2 * width :]
    xproj_w, dt_w, dt_b, _ = lax.optimization_barrier((xproj_weight, dt_weight, dt_bias, normed))
    proj_cols = xproj_w.shape[1]
    small = jnp.concatenate((xproj_w.T, dt_w, dt_b[None]), axis=0)
    copies = jnp.broadcast_to(small[None], (seq_count,) + small.shape)
    small_all = lax.all_to_all(copies, seq, split_axis=0, concat_axis=0, tiled=True)
    xproj_full = jnp.swapaxes(small_all[:, :proj_cols], 1, 2).reshape(total_inner, proj_cols)
    dt_full = jnp.swapaxes(small_all[:, proj_cols : proj_cols + RANK], 0, 1).reshape(
        RANK, total_inner
    )
    dt_bias_full = small_all[:, proj_cols + RANK].reshape(total_inner)
    w_flat, xproj_full, dt_full, dt_bias_full = lax.optimization_barrier(
        (w_flat, xproj_full, dt_full, dt_bias_full)
    )
    both = jnp.dot(normed_all, w_flat, preferred_element_type=jnp.float32)
    w_late, _ = lax.optimization_barrier((w_out_t, normed_all))
    w_col = lax.all_gather(w_late.T, "sz", axis=0, tiled=False)
    xin = both[:, :width]
    zgate = both[:, width:].astype(jnp.bfloat16)
    z_grid = lax.all_to_all(
        zgate.reshape(rows_n, span // rows_n, width), "sz", split_axis=0, concat_axis=0, tiled=True
    )
    padded = jnp.pad(xin, ((taps_count - 1, 0), (0, 0)))
    taps = conv_weight.astype(jnp.float32)
    convolved = conv_bias.astype(jnp.float32) + jnp.zeros_like(xin)
    for tap in range(taps_count):
        convolved = convolved + taps[tap] * padded[tap : tap + span, :]
    inner = jax.nn.silu(convolved).astype(jnp.bfloat16)
    inner_tok = lax.all_to_all(inner, seq, split_axis=0, concat_axis=1, tiled=True)
    proj = jnp.dot(inner_tok, xproj_full, preferred_element_type=jnp.float32)
    length_here = lax.dynamic_index_in_dim(lengths, req_index, 0, keepdims=False)
    positions = seq_index * rows + jnp.arange(rows, dtype=jnp.int32)
    live = (positions < length_here).astype(jnp.float32)
    rate_low = proj[:, :RANK].astype(jnp.bfloat16)
    delta_tok = (
        jax.nn.softplus(
            jnp.dot(rate_low, dt_full, preferred_element_type=jnp.float32)
            + dt_bias_full.astype(jnp.float32)
        )
        * live[:, None]
    )
    decay = -jnp.exp(a_log)
    lanes = 128
    groups = total_inner // lanes
    inner_f = inner_tok.astype(jnp.float32)
    into = proj[:, RANK : RANK + STATE].reshape(-1)
    outof = proj[:, RANK + STATE :].reshape(-1)
    rate_l = delta_tok.reshape(rows, groups, lanes)
    value_l = inner_f.reshape(rows, groups, lanes)
    decay_l = decay.reshape(state_count, groups, lanes)
    skip_l = skip_gain.reshape(groups, lanes)
    end_l, total_l = run_scan(
        False, into, outof, rate_l, value_l, decay_l,
        jnp.zeros((state_count, groups, lanes), jnp.float32), skip_l,
    )
    pair = jnp.concatenate(
        (end_l.reshape(state_count, total_inner), total_l.reshape(1, total_inner))
    ).reshape(state_count + 1, seq_count, width)
    pair_ch = lax.all_to_all(
        jnp.swapaxes(pair, 0, 1), seq, split_axis=0, concat_axis=0, tiled=True
    )
    decay_ch = lax.dynamic_slice_in_dim(decay, seq_index * width, width, 1)
    carry_ch, carry = run_combine(pair_ch, decay_ch)
    carry_in = lax.all_to_all(carry_ch, seq, split_axis=0, concat_axis=0, tiled=True)
    carry_in = jnp.swapaxes(carry_in, 0, 1).reshape(state_count, total_inner)
    out_l = run_scan(
        True, into, outof, rate_l, value_l, decay_l,
        carry_in.reshape(state_count, groups, lanes), skip_l,
    )
    scanned = out_l.reshape(rows, rows_n, cols_n, width).astype(jnp.bfloat16)
    scanned_grid = lax.all_to_all(scanned, "sy", split_axis=2, concat_axis=0, tiled=True)
    z_here = z_grid.reshape(rows_n, cols_n, rows, width).transpose(1, 2, 0, 3)
    gated = (
        scanned_grid.reshape(cols_n, rows, rows_n, width).astype(jnp.float32)
        * jax.nn.silu(z_here.astype(jnp.float32))
    ).astype(jnp.bfloat16)
    partial = jnp.einsum(
        "ktac,acd->ktd", gated, w_col, preferred_element_type=jnp.float32
    ).astype(jnp.bfloat16)
    branch = lax.psum_scatter(
        partial.reshape(cols_n * rows, model), "sy", scatter_dimension=0, tiled=True
    ).astype(jnp.float32)
    slot_all = gather_a2a(carry[None], "req", 0)
    picked = (slot_request == req_index).astype(jnp.float32)
    final_state = jnp.sum(picked[:, None, None] * slot_all, axis=0, keepdims=True)
    mixed = (tokens + branch).astype(jnp.bfloat16)[None]
    return (mixed, final_state)


def solution(mesh):
    seq_n = mesh.shape["seq"]
    rows_n = 1
    while rows_n * rows_n < seq_n:
        rows_n *= 2
    grid = Mesh(mesh.devices.reshape(mesh.shape["req"], rows_n, seq_n // rows_n), ("req", "sz", "sy"))
    seq = ("sz", "sy")
    in_specs = (
        P("req", seq, None),
        P(),
        P(),
        P(),
        P(None, "req", seq),
        P(None, seq),
        P(seq),
        P(seq, None),
        P(None, seq),
        P(seq),
        P(),
        P(),
        P(seq, "req"),
    )
    out_specs = (P("req", seq, None), P("req", None, seq))
    return jax.shard_map(
        per_device, mesh=grid, in_specs=in_specs, out_specs=out_specs, check_vma=False
    )
```

```python
import functools

import jax
import jax.numpy as jnp
from jax import lax
from jax.experimental import pallas as pl
from jax.experimental.pallas import tpu as pltpu
from jax.sharding import Mesh, PartitionSpec as P

STATE = 16
RANK = 128


def gather_a2a(block, axis, dim):
    count = lax.axis_size(axis)
    copies = jnp.broadcast_to(block[None], (count,) + block.shape)
    stacked = lax.all_to_all(copies, axis, split_axis=0, concat_axis=0, tiled=True)
    moved = jnp.moveaxis(stacked, 0, dim)
    shape = list(block.shape)
    shape[dim] = shape[dim] * count
    return moved.reshape(shape)


LANES = 128
SUB = 8


def scan_body(emit, into_ref, outof_ref, rate_ref, value_ref, decay_ref, start_ref, skip_ref, *outs):
    steps = rate_ref.shape[0]
    states = decay_ref.shape[0]
    decay = [decay_ref[n] for n in range(states)]
    if emit:
        out_ref, = outs
        skip = skip_ref[...]
    else:
        end_ref, total_ref = outs

    def step(t, carry):
        held, acc = carry
        rate = rate_ref[t]
        value = value_ref[t]
        push = rate * value
        row = t * states
        new = []
        result = skip * value if emit else None
        for n in range(states):
            s = jnp.exp(rate * decay[n]) * held[n] + push * into_ref[row + n]
            if emit:
                result = result + outof_ref[row + n] * s
            new.append(s)
        if emit:
            out_ref[t] = result
        else:
            acc = acc + rate
        return (tuple(new), acc)

    held0 = tuple(start_ref[n] for n in range(states))
    acc0 = jnp.zeros((SUB, LANES), jnp.float32)
    held, acc = lax.fori_loop(0, steps, step, (held0, acc0), unroll=4)
    if not emit:
        for n in range(states):
            end_ref[n] = held[n]
        total_ref[0] = acc


def run_scan(emit, into, outof, rate, value, decay, start, skip):
    steps, rows, lanes = rate.shape
    states = decay.shape[0]
    chunks = rows // SUB
    smem = pl.BlockSpec(memory_space=pltpu.MemorySpace.SMEM)
    seq_spec = pl.BlockSpec((steps, SUB, lanes), lambda i: (0, i, 0))
    st_spec = pl.BlockSpec((states, SUB, lanes), lambda i: (0, i, 0))
    skip_spec = pl.BlockSpec((SUB, lanes), lambda i: (i, 0))
    if emit:
        out_shape = jax.ShapeDtypeStruct((steps, rows, lanes), jnp.float32)
        out_specs = seq_spec
    else:
        out_shape = (
            jax.ShapeDtypeStruct((states, rows, lanes), jnp.float32),
            jax.ShapeDtypeStruct((1, rows, lanes), jnp.float32),
        )
        out_specs = (st_spec, pl.BlockSpec((1, SUB, lanes), lambda i: (0, i, 0)))
    flops = steps * rows * lanes * states * 6
    return pl.pallas_call(
        functools.partial(scan_body, emit),
        grid=(chunks,),
        in_specs=[smem, smem, seq_spec, seq_spec, st_spec, st_spec, skip_spec],
        out_specs=out_specs,
        out_shape=out_shape,
        cost_estimate=pl.CostEstimate(
            flops=flops,
            transcendentals=steps * rows * lanes * states,
            bytes_accessed=(3 if emit else 2) * steps * rows * lanes * 4,
        ),
    )(into, outof, rate, value, decay, start, skip)


def combine_body(pair_ref, decay_ref, carries_ref, final_ref):
    blocks = pair_ref.shape[0]
    states = decay_ref.shape[0]
    decay = decay_ref[...]
    carry = jnp.zeros(decay.shape, jnp.float32)
    for block in range(blocks):
        carries_ref[block] = carry
        rows = pair_ref[block]
        carry = jnp.exp(rows[states : states + 1] * decay) * carry + rows[:states]
    final_ref[...] = carry


def run_combine(pair, decay):
    blocks = pair.shape[0]
    states, width = decay.shape
    vmem = pl.BlockSpec(memory_space=pltpu.MemorySpace.VMEM)
    return pl.pallas_call(
        combine_body,
        in_specs=[vmem, vmem],
        out_specs=(vmem, vmem),
        out_shape=(
            jax.ShapeDtypeStruct((blocks, states, width), jnp.float32),
            jax.ShapeDtypeStruct((states, width), jnp.float32),
        ),
    )(pair, decay)


def per_device(
    hidden,
    lengths,
    slot_request,
    norm_gain,
    in_weight,
    conv_weight,
    conv_bias,
    xproj_weight,
    dt_weight,
    dt_bias,
    a_log,
    skip_gain,
    out_weight,
):
    seq = ("sz", "sy")
    rows_n = lax.axis_size("sz")
    cols_n = lax.axis_size("sy")
    seq_count = rows_n * cols_n
    seq_index = lax.axis_index(seq)
    req_index = lax.axis_index("req")
    rows = hidden.shape[1]
    span = rows * seq_count
    width = in_weight.shape[2]
    taps_count = conv_weight.shape[0]
    state_count = a_log.shape[0]
    total_inner = a_log.shape[1]
    model = hidden.shape[2]
    tokens = hidden[0].astype(jnp.float32)
    scale = lax.rsqrt(jnp.mean(tokens * tokens, axis=-1, keepdims=True) + 1e-05)
    normed = (tokens * scale * norm_gain.astype(jnp.float32)).astype(jnp.bfloat16)
    normed_all = lax.all_gather(normed, seq, axis=0, tiled=True)
    pieces = jnp.concatenate((in_weight[0], in_weight[1], out_weight.T), axis=1)
    pieces_all = gather_a2a(pieces, "req", 0)
    w_flat = pieces_all[:, : 2 * width]
    w_out_t = pieces_all[:, 2 * width :]
    proj_cols = xproj_weight.shape[1]
    small = jnp.concatenate((xproj_weight.T, dt_weight, dt_bias[None]), axis=0)
    small_late, _ = lax.optimization_barrier((small, normed_all))
    small_all = lax.all_gather(small_late, seq, axis=0, tiled=False)
    xproj_g = small_all[:, :proj_cols]
    dt_g = small_all[:, proj_cols : proj_cols + RANK]
    dt_bias_full = small_all[:, proj_cols + RANK].reshape(total_inner)
    both = jnp.dot(normed_all, w_flat, preferred_element_type=jnp.float32)
    w_late, _ = lax.optimization_barrier((w_out_t, small_all))
    w_col = lax.all_gather(w_late.T, "sz", axis=0, tiled=False)
    xin = both[:, :width]
    zgate = both[:, width:].astype(jnp.bfloat16)
    z_grid = lax.all_to_all(
        zgate.reshape(rows_n, span // rows_n, width), "sz", split_axis=0, concat_axis=0, tiled=True
    )
    padded = jnp.pad(xin, ((taps_count - 1, 0), (0, 0)))
    taps = conv_weight.astype(jnp.float32)
    convolved = conv_bias.astype(jnp.float32) + jnp.zeros_like(xin)
    for tap in range(taps_count):
        convolved = convolved + taps[tap] * padded[tap : tap + span, :]
    inner = jax.nn.silu(convolved).astype(jnp.bfloat16)
    inner_tok = lax.all_to_all(inner, seq, split_axis=0, concat_axis=1, tiled=True)
    proj = jnp.einsum(
        "tsc,skc->tk", inner_tok.reshape(rows, seq_count, width), xproj_g,
        preferred_element_type=jnp.float32,
    )
    length_here = lax.dynamic_index_in_dim(lengths, req_index, 0, keepdims=False)
    positions = seq_index * rows + jnp.arange(rows, dtype=jnp.int32)
    live = (positions < length_here).astype(jnp.float32)
    rate_low = proj[:, :RANK].astype(jnp.bfloat16)
    delta_tok = (
        jax.nn.softplus(
            jnp.einsum("tk,skc->tsc", rate_low, dt_g, preferred_element_type=jnp.float32).reshape(
                rows, total_inner
            )
            + dt_bias_full.astype(jnp.float32)
        )
        * live[:, None]
    )
    decay = -jnp.exp(a_log)
    lanes = 128
    groups = total_inner // lanes
    inner_f = inner_tok.astype(jnp.float32)
    into = proj[:, RANK : RANK + STATE].reshape(-1)
    outof = proj[:, RANK + STATE :].reshape(-1)
    rate_l = delta_tok.reshape(rows, groups, lanes)
    value_l = inner_f.reshape(rows, groups, lanes)
    decay_l = decay.reshape(state_count, groups, lanes)
    skip_l = skip_gain.reshape(groups, lanes)
    end_l, total_l = run_scan(
        False, into, outof, rate_l, value_l, decay_l,
        jnp.zeros((state_count, groups, lanes), jnp.float32), skip_l,
    )
    pair = jnp.concatenate(
        (end_l.reshape(state_count, total_inner), total_l.reshape(1, total_inner))
    ).reshape(state_count + 1, seq_count, width)
    pair_ch = lax.all_to_all(
        jnp.swapaxes(pair, 0, 1), seq, split_axis=0, concat_axis=0, tiled=True
    )
    decay_ch = lax.dynamic_slice_in_dim(decay, seq_index * width, width, 1)
    carry_ch, carry = run_combine(pair_ch, decay_ch)
    carry_in = lax.all_to_all(carry_ch, seq, split_axis=0, concat_axis=0, tiled=True)
    carry_in = jnp.swapaxes(carry_in, 0, 1).reshape(state_count, total_inner)
    out_l = run_scan(
        True, into, outof, rate_l, value_l, decay_l,
        carry_in.reshape(state_count, groups, lanes), skip_l,
    )
    scanned = out_l.reshape(rows, rows_n, cols_n, width).astype(jnp.bfloat16)
    scanned_grid = lax.all_to_all(scanned, "sy", split_axis=2, concat_axis=0, tiled=True)
    z_here = z_grid.reshape(rows_n, cols_n, rows, width).transpose(1, 2, 0, 3)
    gated = (
        scanned_grid.reshape(cols_n, rows, rows_n, width).astype(jnp.float32)
        * jax.nn.silu(z_here.astype(jnp.float32))
    ).astype(jnp.bfloat16)
    partial = jnp.einsum(
        "ktac,acd->ktd", gated, w_col, preferred_element_type=jnp.float32
    ).astype(jnp.bfloat16)
    branch = lax.psum_scatter(
        partial.reshape(cols_n * rows, model), "sy", scatter_dimension=0, tiled=True
    ).astype(jnp.float32)
    slot_all = gather_a2a(carry[None], "req", 0)
    picked = (slot_request == req_index).astype(jnp.float32)
    final_state = jnp.sum(picked[:, None, None] * slot_all, axis=0, keepdims=True)
    mixed = (tokens + branch).astype(jnp.bfloat16)[None]
    return (mixed, final_state)


def solution(mesh):
    seq_n = mesh.shape["seq"]
    rows_n = 1
    while rows_n * rows_n < seq_n:
        rows_n *= 2
    grid = Mesh(mesh.devices.reshape(mesh.shape["req"], rows_n, seq_n // rows_n), ("req", "sz", "sy"))
    seq = ("sz", "sy")
    in_specs = (
        P("req", seq, None),
        P(),
        P(),
        P(),
        P(None, "req", seq),
        P(None, seq),
        P(seq),
        P(seq, None),
        P(None, seq),
        P(seq),
        P(),
        P(),
        P(seq, "req"),
    )
    out_specs = (P("req", seq, None), P("req", None, seq))
    return jax.shard_map(
        per_device, mesh=grid, in_specs=in_specs, out_specs=out_specs, check_vma=False
    )
```

```python
import functools

import jax
import jax.numpy as jnp
from jax import lax
from jax.experimental import pallas as pl
from jax.experimental.pallas import tpu as pltpu
from jax.sharding import Mesh, PartitionSpec as P

STATE = 16
RANK = 128


def gather_a2a(block, axis, dim):
    count = lax.axis_size(axis)
    copies = jnp.broadcast_to(block[None], (count,) + block.shape)
    stacked = lax.all_to_all(copies, axis, split_axis=0, concat_axis=0, tiled=True)
    moved = jnp.moveaxis(stacked, 0, dim)
    shape = list(block.shape)
    shape[dim] = shape[dim] * count
    return moved.reshape(shape)


LANES = 128
SUB = 8


def scan_body(emit, into_ref, outof_ref, rate_ref, value_ref, decay_ref, start_ref, skip_ref, *outs):
    steps = rate_ref.shape[0]
    states = decay_ref.shape[0]
    decay = [decay_ref[n] for n in range(states)]
    if emit:
        out_ref, = outs
        skip = skip_ref[...]
    else:
        end_ref, total_ref = outs

    def step(t, carry):
        held, acc = carry
        rate = rate_ref[t]
        value = value_ref[t]
        push = rate * value
        row = t * states
        new = []
        result = skip * value if emit else None
        for n in range(states):
            s = jnp.exp(rate * decay[n]) * held[n] + push * into_ref[row + n]
            if emit:
                result = result + outof_ref[row + n] * s
            new.append(s)
        if emit:
            out_ref[t] = result
        else:
            acc = acc + rate
        return (tuple(new), acc)

    held0 = tuple(start_ref[n] for n in range(states))
    acc0 = jnp.zeros((SUB, LANES), jnp.float32)
    held, acc = lax.fori_loop(0, steps, step, (held0, acc0), unroll=4)
    if not emit:
        for n in range(states):
            end_ref[n] = held[n]
        total_ref[0] = acc


def run_scan(emit, into, outof, rate, value, decay, start, skip):
    steps, rows, lanes = rate.shape
    states = decay.shape[0]
    chunks = rows // SUB
    smem = pl.BlockSpec(memory_space=pltpu.MemorySpace.SMEM)
    seq_spec = pl.BlockSpec((steps, SUB, lanes), lambda i: (0, i, 0))
    st_spec = pl.BlockSpec((states, SUB, lanes), lambda i: (0, i, 0))
    skip_spec = pl.BlockSpec((SUB, lanes), lambda i: (i, 0))
    if emit:
        out_shape = jax.ShapeDtypeStruct((steps, rows, lanes), jnp.float32)
        out_specs = seq_spec
    else:
        out_shape = (
            jax.ShapeDtypeStruct((states, rows, lanes), jnp.float32),
            jax.ShapeDtypeStruct((1, rows, lanes), jnp.float32),
        )
        out_specs = (st_spec, pl.BlockSpec((1, SUB, lanes), lambda i: (0, i, 0)))
    flops = steps * rows * lanes * states * 6
    return pl.pallas_call(
        functools.partial(scan_body, emit),
        grid=(chunks,),
        in_specs=[smem, smem, seq_spec, seq_spec, st_spec, st_spec, skip_spec],
        out_specs=out_specs,
        out_shape=out_shape,
        cost_estimate=pl.CostEstimate(
            flops=flops,
            transcendentals=steps * rows * lanes * states,
            bytes_accessed=(3 if emit else 2) * steps * rows * lanes * 4,
        ),
    )(into, outof, rate, value, decay, start, skip)


def combine_body(pair_ref, decay_ref, carries_ref, final_ref):
    blocks = pair_ref.shape[0]
    states = decay_ref.shape[0]
    decay = decay_ref[...]
    carry = jnp.zeros(decay.shape, jnp.float32)
    for block in range(blocks):
        carries_ref[block] = carry
        rows = pair_ref[block]
        carry = jnp.exp(rows[states : states + 1] * decay) * carry + rows[:states]
    final_ref[...] = carry


def run_combine(pair, decay):
    blocks = pair.shape[0]
    states, width = decay.shape
    vmem = pl.BlockSpec(memory_space=pltpu.MemorySpace.VMEM)
    return pl.pallas_call(
        combine_body,
        in_specs=[vmem, vmem],
        out_specs=(vmem, vmem),
        out_shape=(
            jax.ShapeDtypeStruct((blocks, states, width), jnp.float32),
            jax.ShapeDtypeStruct((states, width), jnp.float32),
        ),
    )(pair, decay)


def per_device(
    hidden,
    lengths,
    slot_request,
    norm_gain,
    in_weight,
    conv_weight,
    conv_bias,
    xproj_weight,
    dt_weight,
    dt_bias,
    a_log,
    skip_gain,
    out_weight,
):
    seq = ("sz", "sy")
    rows_n = lax.axis_size("sz")
    cols_n = lax.axis_size("sy")
    seq_count = rows_n * cols_n
    seq_index = lax.axis_index(seq)
    req_index = lax.axis_index("req")
    rows = hidden.shape[1]
    span = rows * seq_count
    width = in_weight.shape[2]
    taps_count = conv_weight.shape[0]
    state_count = a_log.shape[0]
    total_inner = a_log.shape[1]
    model = hidden.shape[2]
    tokens = hidden[0].astype(jnp.float32)
    scale = lax.rsqrt(jnp.mean(tokens * tokens, axis=-1, keepdims=True) + 1e-05)
    normed = (tokens * scale * norm_gain.astype(jnp.float32)).astype(jnp.bfloat16)
    normed_all = lax.all_gather(normed, seq, axis=0, tiled=True)
    pieces = jnp.concatenate((in_weight, out_weight.T[None]), axis=0)
    pieces_all = gather_a2a(pieces, "req", 1)
    w_in = pieces_all[:2]
    w_out_t = pieces_all[2]
    xproj_w, dt_w, dt_b, _ = lax.optimization_barrier((xproj_weight, dt_weight, dt_bias, normed))
    proj_cols = xproj_w.shape[1]
    small = jnp.concatenate((xproj_w.T, dt_w, dt_b[None]), axis=0)
    copies = jnp.broadcast_to(small[None], (seq_count,) + small.shape)
    small_all = lax.all_to_all(copies, seq, split_axis=0, concat_axis=0, tiled=True)
    xproj_full = small_all[:, :proj_cols]
    dt_full = small_all[:, proj_cols : proj_cols + RANK]
    dt_bias_full = small_all[:, proj_cols + RANK].reshape(total_inner)
    w_in, xproj_full, dt_full, dt_bias_full = lax.optimization_barrier(
        (w_in, xproj_full, dt_full, dt_bias_full)
    )
    w_flat = jnp.concatenate((w_in[0], w_in[1]), axis=1)
    both = jnp.dot(normed_all, w_flat, preferred_element_type=jnp.float32)
    w_late, _ = lax.optimization_barrier((w_out_t, normed_all))
    w_col = lax.all_gather(w_late.T, "sz", axis=0, tiled=False)
    xin = both[:, :width]
    zgate = both[:, width:].astype(jnp.bfloat16)
    z_grid = lax.all_to_all(
        zgate.reshape(rows_n, span // rows_n, width), "sz", split_axis=0, concat_axis=0, tiled=True
    )
    padded = jnp.pad(xin, ((taps_count - 1, 0), (0, 0)))
    taps = conv_weight.astype(jnp.float32)
    convolved = conv_bias.astype(jnp.float32) + jnp.zeros_like(xin)
    for tap in range(taps_count):
        convolved = convolved + taps[tap] * padded[tap : tap + span, :]
    inner = jax.nn.silu(convolved).astype(jnp.bfloat16)
    inner_tok = lax.all_to_all(inner, seq, split_axis=0, concat_axis=1, tiled=True)
    proj = jnp.einsum(
        "tsc,skc->tk", inner_tok.reshape(rows, seq_count, width), xproj_full,
        preferred_element_type=jnp.float32,
    )
    length_here = lax.dynamic_index_in_dim(lengths, req_index, 0, keepdims=False)
    positions = seq_index * rows + jnp.arange(rows, dtype=jnp.int32)
    live = (positions < length_here).astype(jnp.float32)
    rate_low = proj[:, :RANK].astype(jnp.bfloat16)
    delta_tok = (
        jax.nn.softplus(
            jnp.einsum(
                "tk,skc->tsc", rate_low, dt_full, preferred_element_type=jnp.float32
            ).reshape(rows, total_inner)
            + dt_bias_full.astype(jnp.float32)
        )
        * live[:, None]
    )
    decay = -jnp.exp(a_log)
    lanes = 128
    groups = total_inner // lanes
    inner_f = inner_tok.astype(jnp.float32)
    into = proj[:, RANK : RANK + STATE].reshape(-1)
    outof = proj[:, RANK + STATE :].reshape(-1)
    rate_l = delta_tok.reshape(rows, groups, lanes)
    value_l = inner_f.reshape(rows, groups, lanes)
    decay_l = decay.reshape(state_count, groups, lanes)
    skip_l = skip_gain.reshape(groups, lanes)
    end_l, total_l = run_scan(
        False, into, outof, rate_l, value_l, decay_l,
        jnp.zeros((state_count, groups, lanes), jnp.float32), skip_l,
    )
    pair = jnp.concatenate(
        (end_l.reshape(state_count, total_inner), total_l.reshape(1, total_inner))
    ).reshape(state_count + 1, seq_count, width)
    pair_ch = lax.all_to_all(
        jnp.swapaxes(pair, 0, 1), seq, split_axis=0, concat_axis=0, tiled=True
    )
    decay_ch = lax.dynamic_slice_in_dim(decay, seq_index * width, width, 1)
    carry_ch, carry = run_combine(pair_ch, decay_ch)
    carry_in = lax.all_to_all(carry_ch, seq, split_axis=0, concat_axis=0, tiled=True)
    carry_in = jnp.swapaxes(carry_in, 0, 1).reshape(state_count, total_inner)
    out_l = run_scan(
        True, into, outof, rate_l, value_l, decay_l,
        carry_in.reshape(state_count, groups, lanes), skip_l,
    )
    scanned = out_l.reshape(rows, rows_n, cols_n, width).astype(jnp.bfloat16)
    scanned_grid = lax.all_to_all(scanned, "sy", split_axis=2, concat_axis=0, tiled=True)
    z_here = z_grid.reshape(rows_n, cols_n, rows, width).transpose(1, 2, 0, 3)
    gated = (
        scanned_grid.reshape(cols_n, rows, rows_n, width).astype(jnp.float32)
        * jax.nn.silu(z_here.astype(jnp.float32))
    ).astype(jnp.bfloat16)
    partial = jnp.einsum(
        "ktac,acd->ktd", gated, w_col, preferred_element_type=jnp.float32
    ).astype(jnp.bfloat16)
    branch = lax.psum_scatter(
        partial.reshape(cols_n * rows, model), "sy", scatter_dimension=0, tiled=True
    ).astype(jnp.float32)
    slot_all = gather_a2a(carry[None], "req", 0)
    picked = (slot_request == req_index).astype(jnp.float32)
    final_state = jnp.sum(picked[:, None, None] * slot_all, axis=0, keepdims=True)
    mixed = (tokens + branch).astype(jnp.bfloat16)[None]
    return (mixed, final_state)


def solution(mesh):
    seq_n = mesh.shape["seq"]
    rows_n = 1
    while rows_n * rows_n < seq_n:
        rows_n *= 2
    grid = Mesh(mesh.devices.reshape(mesh.shape["req"], rows_n, seq_n // rows_n), ("req", "sz", "sy"))
    seq = ("sz", "sy")
    in_specs = (
        P("req", seq, None),
        P(),
        P(),
        P(),
        P(None, "req", seq),
        P(None, seq),
        P(seq),
        P(seq, None),
        P(None, seq),
        P(seq),
        P(),
        P(),
        P(seq, "req"),
    )
    out_specs = (P("req", seq, None), P("req", None, seq))
    return jax.shard_map(
        per_device, mesh=grid, in_specs=in_specs, out_specs=out_specs, check_vma=False
    )
```

```python
import functools

import jax
import jax.numpy as jnp
from jax import lax
from jax.experimental import pallas as pl
from jax.experimental.pallas import tpu as pltpu
from jax.sharding import Mesh, PartitionSpec as P

STATE = 16
RANK = 128


def gather_a2a(block, axis, dim):
    count = lax.axis_size(axis)
    copies = jnp.broadcast_to(block[None], (count,) + block.shape)
    stacked = lax.all_to_all(copies, axis, split_axis=0, concat_axis=0, tiled=True)
    moved = jnp.moveaxis(stacked, 0, dim)
    shape = list(block.shape)
    shape[dim] = shape[dim] * count
    return moved.reshape(shape)


LANES = 128
SUB = 8


def scan_body(emit, into_ref, outof_ref, rate_ref, value_ref, decay_ref, start_ref, skip_ref, *outs):
    steps = rate_ref.shape[0]
    states = decay_ref.shape[0]
    decay = [decay_ref[n] for n in range(states)]
    if emit:
        out_ref, = outs
        skip = skip_ref[...]
    else:
        end_ref, total_ref = outs

    def step(t, carry):
        held, acc = carry
        rate = rate_ref[t]
        value = value_ref[t]
        push = rate * value
        row = t * states
        new = []
        result = skip * value if emit else None
        for n in range(states):
            s = jnp.exp(rate * decay[n]) * held[n] + push * into_ref[row + n]
            if emit:
                result = result + outof_ref[row + n] * s
            new.append(s)
        if emit:
            out_ref[t] = result
        else:
            acc = acc + rate
        return (tuple(new), acc)

    held0 = tuple(start_ref[n] for n in range(states))
    acc0 = jnp.zeros((SUB, LANES), jnp.float32)
    held, acc = lax.fori_loop(0, steps, step, (held0, acc0), unroll=2)
    if not emit:
        for n in range(states):
            end_ref[n] = held[n]
        total_ref[0] = acc


def run_scan(emit, into, outof, rate, value, decay, start, skip):
    steps, rows, lanes = rate.shape
    states = decay.shape[0]
    chunks = rows // SUB
    smem = pl.BlockSpec(memory_space=pltpu.MemorySpace.SMEM)
    seq_spec = pl.BlockSpec((steps, SUB, lanes), lambda i: (0, i, 0))
    st_spec = pl.BlockSpec((states, SUB, lanes), lambda i: (0, i, 0))
    skip_spec = pl.BlockSpec((SUB, lanes), lambda i: (i, 0))
    if emit:
        out_shape = jax.ShapeDtypeStruct((steps, rows, lanes), jnp.float32)
        out_specs = seq_spec
    else:
        out_shape = (
            jax.ShapeDtypeStruct((states, rows, lanes), jnp.float32),
            jax.ShapeDtypeStruct((1, rows, lanes), jnp.float32),
        )
        out_specs = (st_spec, pl.BlockSpec((1, SUB, lanes), lambda i: (0, i, 0)))
    flops = steps * rows * lanes * states * 6
    return pl.pallas_call(
        functools.partial(scan_body, emit),
        grid=(chunks,),
        in_specs=[smem, smem, seq_spec, seq_spec, st_spec, st_spec, skip_spec],
        out_specs=out_specs,
        out_shape=out_shape,
        cost_estimate=pl.CostEstimate(
            flops=flops,
            transcendentals=steps * rows * lanes * states,
            bytes_accessed=(3 if emit else 2) * steps * rows * lanes * 4,
        ),
    )(into, outof, rate, value, decay, start, skip)


def combine_body(pair_ref, decay_ref, carries_ref, final_ref):
    blocks = pair_ref.shape[0]
    states = decay_ref.shape[0]
    decay = decay_ref[...]
    carry = jnp.zeros(decay.shape, jnp.float32)
    for block in range(blocks):
        carries_ref[block] = carry
        rows = pair_ref[block]
        carry = jnp.exp(rows[states : states + 1] * decay) * carry + rows[:states]
    final_ref[...] = carry


def run_combine(pair, decay):
    blocks = pair.shape[0]
    states, width = decay.shape
    vmem = pl.BlockSpec(memory_space=pltpu.MemorySpace.VMEM)
    return pl.pallas_call(
        combine_body,
        in_specs=[vmem, vmem],
        out_specs=(vmem, vmem),
        out_shape=(
            jax.ShapeDtypeStruct((blocks, states, width), jnp.float32),
            jax.ShapeDtypeStruct((states, width), jnp.float32),
        ),
    )(pair, decay)


def per_device(
    hidden,
    lengths,
    slot_request,
    norm_gain,
    in_weight,
    conv_weight,
    conv_bias,
    xproj_weight,
    dt_weight,
    dt_bias,
    a_log,
    skip_gain,
    out_weight,
):
    seq = ("sz", "sy")
    rows_n = lax.axis_size("sz")
    cols_n = lax.axis_size("sy")
    seq_count = rows_n * cols_n
    seq_index = lax.axis_index(seq)
    req_index = lax.axis_index(("rx", "rc"))
    rows = hidden.shape[1]
    span = rows * seq_count
    width = in_weight.shape[2]
    taps_count = conv_weight.shape[0]
    state_count = a_log.shape[0]
    total_inner = a_log.shape[1]
    model = hidden.shape[2]
    tokens = hidden[0].astype(jnp.float32)
    scale = lax.rsqrt(jnp.mean(tokens * tokens, axis=-1, keepdims=True) + 1e-05)
    normed = (tokens * scale * norm_gain.astype(jnp.float32)).astype(jnp.bfloat16)
    normed_all = lax.all_gather(normed, seq, axis=0, tiled=True)
    pieces = jnp.concatenate((in_weight, out_weight.T[None]), axis=0)
    pieces_row = gather_a2a(pieces[None], "rx", 0)
    pieces_pair = gather_a2a(pieces_row[None], "rc", 0)
    pieces_all = jnp.moveaxis(
        jnp.swapaxes(pieces_pair, 0, 1).reshape((-1,) + pieces.shape), 0, 1
    ).reshape((pieces.shape[0], -1) + pieces.shape[2:])
    w_in = pieces_all[:2]
    w_out_t = pieces_all[2]
    xproj_w, dt_w, dt_b, _ = lax.optimization_barrier((xproj_weight, dt_weight, dt_bias, normed))
    proj_cols = xproj_w.shape[1]
    small = jnp.concatenate((xproj_w.T, dt_w, dt_b[None]), axis=0)
    lane_half = width // 2
    core = lax.axis_index("rc")
    mine = lax.dynamic_slice_in_dim(small, core * lane_half, lane_half, 1)
    copies = jnp.broadcast_to(mine[None], (seq_count,) + mine.shape)
    half_all = lax.all_to_all(copies, seq, split_axis=0, concat_axis=0, tiled=True)
    both_halves = gather_a2a(half_all[None], "rc", 0)
    small_all = jnp.moveaxis(both_halves, 0, 2).reshape(half_all.shape[:2] + (width,))
    xproj_full = jnp.swapaxes(small_all[:, :proj_cols], 1, 2).reshape(total_inner, proj_cols)
    dt_full = jnp.swapaxes(small_all[:, proj_cols : proj_cols + RANK], 0, 1).reshape(
        RANK, total_inner
    )
    dt_bias_full = small_all[:, proj_cols + RANK].reshape(total_inner)
    w_in, xproj_full, dt_full, dt_bias_full = lax.optimization_barrier(
        (w_in, xproj_full, dt_full, dt_bias_full)
    )
    w_flat = jnp.concatenate((w_in[0], w_in[1]), axis=1)
    both = jnp.dot(normed_all, w_flat, preferred_element_type=jnp.float32)
    w_late, _ = lax.optimization_barrier((w_out_t, normed_all))
    w_col = lax.all_gather(w_late.T, "sz", axis=0, tiled=False)
    xin = both[:, :width]
    zgate = both[:, width:].astype(jnp.bfloat16)
    z_grid = lax.all_to_all(
        zgate.reshape(rows_n, span // rows_n, width), "sz", split_axis=0, concat_axis=0, tiled=True
    )
    padded = jnp.pad(xin, ((taps_count - 1, 0), (0, 0)))
    taps = conv_weight.astype(jnp.float32)
    convolved = conv_bias.astype(jnp.float32) + jnp.zeros_like(xin)
    for tap in range(taps_count):
        convolved = convolved + taps[tap] * padded[tap : tap + span, :]
    inner = jax.nn.silu(convolved).astype(jnp.bfloat16)
    inner_tok = lax.all_to_all(inner, seq, split_axis=0, concat_axis=1, tiled=True)
    proj = jnp.dot(inner_tok, xproj_full, preferred_element_type=jnp.float32)
    length_here = lax.dynamic_index_in_dim(lengths, req_index, 0, keepdims=False)
    positions = seq_index * rows + jnp.arange(rows, dtype=jnp.int32)
    live = (positions < length_here).astype(jnp.float32)
    rate_low = proj[:, :RANK].astype(jnp.bfloat16)
    delta_tok = (
        jax.nn.softplus(
            jnp.dot(rate_low, dt_full, preferred_element_type=jnp.float32)
            + dt_bias_full.astype(jnp.float32)
        )
        * live[:, None]
    )
    decay = -jnp.exp(a_log)
    lanes = 128
    groups = total_inner // lanes
    inner_f = inner_tok.astype(jnp.float32)
    into = proj[:, RANK : RANK + STATE].reshape(-1)
    outof = proj[:, RANK + STATE :].reshape(-1)
    rate_l = delta_tok.reshape(rows, groups, lanes)
    value_l = inner_f.reshape(rows, groups, lanes)
    decay_l = decay.reshape(state_count, groups, lanes)
    skip_l = skip_gain.reshape(groups, lanes)
    end_l, total_l = run_scan(
        False, into, outof, rate_l, value_l, decay_l,
        jnp.zeros((state_count, groups, lanes), jnp.float32), skip_l,
    )
    pair = jnp.concatenate(
        (end_l.reshape(state_count, total_inner), total_l.reshape(1, total_inner))
    ).reshape(state_count + 1, seq_count, width)
    pair_ch = lax.all_to_all(
        jnp.swapaxes(pair, 0, 1), seq, split_axis=0, concat_axis=0, tiled=True
    )
    decay_ch = lax.dynamic_slice_in_dim(decay, seq_index * width, width, 1)
    carry_ch, carry = run_combine(pair_ch, decay_ch)
    carry_in = lax.all_to_all(carry_ch, seq, split_axis=0, concat_axis=0, tiled=True)
    carry_in = jnp.swapaxes(carry_in, 0, 1).reshape(state_count, total_inner)
    out_l = run_scan(
        True, into, outof, rate_l, value_l, decay_l,
        carry_in.reshape(state_count, groups, lanes), skip_l,
    )
    scanned = out_l.reshape(rows, rows_n, cols_n, width).astype(jnp.bfloat16)
    scanned_grid = lax.all_to_all(scanned, "sy", split_axis=2, concat_axis=0, tiled=True)
    z_here = z_grid.reshape(rows_n, cols_n, rows, width).transpose(1, 2, 0, 3)
    gated = (
        scanned_grid.reshape(cols_n, rows, rows_n, width).astype(jnp.float32)
        * jax.nn.silu(z_here.astype(jnp.float32))
    ).astype(jnp.bfloat16)
    partial = jnp.einsum(
        "ktac,acd->ktd", gated, w_col, preferred_element_type=jnp.float32
    ).astype(jnp.bfloat16)
    branch = lax.psum_scatter(
        partial.reshape(cols_n * rows, model), "sy", scatter_dimension=0, tiled=True
    ).astype(jnp.float32)
    slot_all = gather_a2a(carry[None], ("rx", "rc"), 0)
    picked = (slot_request == req_index).astype(jnp.float32)
    final_state = jnp.sum(picked[:, None, None] * slot_all, axis=0, keepdims=True)
    mixed = (tokens + branch).astype(jnp.bfloat16)[None]
    return (mixed, final_state)


def solution(mesh):
    seq_n = mesh.shape["seq"]
    rows_n = 1
    while rows_n * rows_n < seq_n:
        rows_n *= 2
    grid = Mesh(
        mesh.devices.reshape(mesh.shape["req"] // 2, 2, rows_n, seq_n // rows_n),
        ("rx", "rc", "sz", "sy"),
    )
    req = ("rx", "rc")
    seq = ("sz", "sy")
    in_specs = (
        P(req, seq, None),
        P(),
        P(),
        P(),
        P(None, req, seq),
        P(None, seq),
        P(seq),
        P(seq, None),
        P(None, seq),
        P(seq),
        P(),
        P(),
        P(seq, req),
    )
    out_specs = (P(req, seq, None), P(req, None, seq))
    return jax.shard_map(
        per_device, mesh=grid, in_specs=in_specs, out_specs=out_specs, check_vma=False
    )
```

```python
import functools

import jax
import jax.numpy as jnp
from jax import lax
from jax.experimental import pallas as pl
from jax.experimental.pallas import tpu as pltpu
from jax.sharding import Mesh, PartitionSpec as P

STATE = 16
RANK = 128


def gather_a2a(block, axis, dim):
    count = lax.axis_size(axis)
    copies = jnp.broadcast_to(block[None], (count,) + block.shape)
    stacked = lax.all_to_all(copies, axis, split_axis=0, concat_axis=0, tiled=True)
    moved = jnp.moveaxis(stacked, 0, dim)
    shape = list(block.shape)
    shape[dim] = shape[dim] * count
    return moved.reshape(shape)


LANES = 128
SUB = 8


def scan_body(emit, into_ref, outof_ref, rate_ref, value_ref, decay_ref, start_ref, skip_ref, *outs):
    steps = rate_ref.shape[0]
    states = decay_ref.shape[0]
    decay = [decay_ref[n] for n in range(states)]
    if emit:
        out_ref, = outs
        skip = skip_ref[...]
    else:
        end_ref, total_ref = outs

    def step(t, carry):
        held, acc = carry
        rate = rate_ref[t]
        value = value_ref[t]
        push = rate * value
        row = t * states
        new = []
        result = skip * value if emit else None
        for n in range(states):
            s = jnp.exp(rate * decay[n]) * held[n] + push * into_ref[row + n]
            if emit:
                result = result + outof_ref[row + n] * s
            new.append(s)
        if emit:
            out_ref[t] = result
        else:
            acc = acc + rate
        return (tuple(new), acc)

    held0 = tuple(start_ref[n] for n in range(states))
    acc0 = jnp.zeros((SUB, LANES), jnp.float32)
    held, acc = lax.fori_loop(0, steps, step, (held0, acc0), unroll=4)
    if not emit:
        for n in range(states):
            end_ref[n] = held[n]
        total_ref[0] = acc


def run_scan(emit, into, outof, rate, value, decay, start, skip):
    steps, rows, lanes = rate.shape
    states = decay.shape[0]
    chunks = rows // SUB
    smem = pl.BlockSpec(memory_space=pltpu.MemorySpace.SMEM)
    seq_spec = pl.BlockSpec((steps, SUB, lanes), lambda i: (0, i, 0))
    st_spec = pl.BlockSpec((states, SUB, lanes), lambda i: (0, i, 0))
    skip_spec = pl.BlockSpec((SUB, lanes), lambda i: (i, 0))
    if emit:
        out_shape = jax.ShapeDtypeStruct((steps, rows, lanes), jnp.float32)
        out_specs = seq_spec
    else:
        out_shape = (
            jax.ShapeDtypeStruct((states, rows, lanes), jnp.float32),
            jax.ShapeDtypeStruct((1, rows, lanes), jnp.float32),
        )
        out_specs = (st_spec, pl.BlockSpec((1, SUB, lanes), lambda i: (0, i, 0)))
    flops = steps * rows * lanes * states * 6
    return pl.pallas_call(
        functools.partial(scan_body, emit),
        grid=(chunks,),
        in_specs=[smem, smem, seq_spec, seq_spec, st_spec, st_spec, skip_spec],
        out_specs=out_specs,
        out_shape=out_shape,
        cost_estimate=pl.CostEstimate(
            flops=flops,
            transcendentals=steps * rows * lanes * states,
            bytes_accessed=(3 if emit else 2) * steps * rows * lanes * 4,
        ),
    )(into, outof, rate, value, decay, start, skip)


def combine_body(pair_ref, decay_ref, carries_ref, final_ref):
    blocks = pair_ref.shape[0]
    states = decay_ref.shape[0]
    decay = decay_ref[...]
    carry = jnp.zeros(decay.shape, jnp.float32)
    for block in range(blocks):
        carries_ref[block] = carry
        rows = pair_ref[block]
        carry = jnp.exp(rows[states : states + 1] * decay) * carry + rows[:states]
    final_ref[...] = carry


def run_combine(pair, decay):
    blocks = pair.shape[0]
    states, width = decay.shape
    vmem = pl.BlockSpec(memory_space=pltpu.MemorySpace.VMEM)
    return pl.pallas_call(
        combine_body,
        in_specs=[vmem, vmem],
        out_specs=(vmem, vmem),
        out_shape=(
            jax.ShapeDtypeStruct((blocks, states, width), jnp.float32),
            jax.ShapeDtypeStruct((states, width), jnp.float32),
        ),
    )(pair, decay)


def per_device(
    hidden,
    lengths,
    slot_request,
    norm_gain,
    in_weight,
    conv_weight,
    conv_bias,
    xproj_weight,
    dt_weight,
    dt_bias,
    a_log,
    skip_gain,
    out_weight,
):
    seq = ("sz", "sy")
    rows_n = lax.axis_size("sz")
    cols_n = lax.axis_size("sy")
    seq_count = rows_n * cols_n
    seq_index = lax.axis_index(seq)
    req_index = lax.axis_index(("rx", "rc"))
    rows = hidden.shape[1]
    span = rows * seq_count
    width = in_weight.shape[2]
    taps_count = conv_weight.shape[0]
    state_count = a_log.shape[0]
    total_inner = a_log.shape[1]
    model = hidden.shape[2]
    tokens = hidden[0].astype(jnp.float32)
    scale = lax.rsqrt(jnp.mean(tokens * tokens, axis=-1, keepdims=True) + 1e-05)
    normed = (tokens * scale * norm_gain.astype(jnp.float32)).astype(jnp.bfloat16)
    normed_all = lax.all_gather(normed, seq, axis=0, tiled=True)
    pieces = jnp.concatenate((in_weight, out_weight.T[None]), axis=0)
    pieces_row = gather_a2a(pieces[None], "rx", 0)
    pieces_pair = gather_a2a(pieces_row[None], "rc", 0)
    pieces_all = jnp.moveaxis(
        jnp.swapaxes(pieces_pair, 0, 1).reshape((-1,) + pieces.shape), 0, 1
    ).reshape((pieces.shape[0], -1) + pieces.shape[2:])
    w_in = pieces_all[:2]
    w_out_t = pieces_all[2]
    xproj_w, dt_w, dt_b, _ = lax.optimization_barrier((xproj_weight, dt_weight, dt_bias, normed))
    proj_cols = xproj_w.shape[1]
    small = jnp.concatenate((xproj_w.T, dt_w, dt_b[None]), axis=0)
    lane_half = width // 2
    core = lax.axis_index("rc")
    mine = lax.dynamic_slice_in_dim(small, core * lane_half, lane_half, 1)
    copies = jnp.broadcast_to(mine[None], (seq_count,) + mine.shape)
    half_all = lax.all_to_all(copies, seq, split_axis=0, concat_axis=0, tiled=True)
    both_halves = gather_a2a(half_all[None], "rc", 0)
    small_all = jnp.moveaxis(both_halves, 0, 2).reshape(half_all.shape[:2] + (width,))
    xproj_full = jnp.swapaxes(small_all[:, :proj_cols], 1, 2).reshape(total_inner, proj_cols)
    dt_full = jnp.swapaxes(small_all[:, proj_cols : proj_cols + RANK], 0, 1).reshape(
        RANK, total_inner
    )
    dt_bias_full = small_all[:, proj_cols + RANK].reshape(total_inner)
    w_in, xproj_full, dt_full, dt_bias_full = lax.optimization_barrier(
        (w_in, xproj_full, dt_full, dt_bias_full)
    )
    w_flat = jnp.concatenate((w_in[0], w_in[1]), axis=1)
    both = jnp.dot(normed_all, w_flat, preferred_element_type=jnp.float32)
    w_late, _ = lax.optimization_barrier((w_out_t, normed_all))
    w_col = lax.all_gather(w_late.T, "sz", axis=0, tiled=False)
    xin = both[:, :width]
    zgate = both[:, width:].astype(jnp.bfloat16)
    z_grid = lax.all_to_all(
        zgate.reshape(rows_n, span // rows_n, width), "sz", split_axis=0, concat_axis=0, tiled=True
    )
    padded = jnp.pad(xin, ((taps_count - 1, 0), (0, 0)))
    taps = conv_weight.astype(jnp.float32)
    convolved = conv_bias.astype(jnp.float32) + jnp.zeros_like(xin)
    for tap in range(taps_count):
        convolved = convolved + taps[tap] * padded[tap : tap + span, :]
    inner = jax.nn.silu(convolved).astype(jnp.bfloat16)
    inner_tok = lax.all_to_all(inner, seq, split_axis=0, concat_axis=1, tiled=True)
    proj = jnp.dot(inner_tok, xproj_full, preferred_element_type=jnp.float32)
    length_here = lax.dynamic_index_in_dim(lengths, req_index, 0, keepdims=False)
    positions = seq_index * rows + jnp.arange(rows, dtype=jnp.int32)
    live = (positions < length_here).astype(jnp.float32)
    rate_low = proj[:, :RANK].astype(jnp.bfloat16)
    delta_tok = (
        jax.nn.softplus(
            jnp.dot(rate_low, dt_full, preferred_element_type=jnp.float32)
            + dt_bias_full.astype(jnp.float32)
        )
        * live[:, None]
    )
    decay = -jnp.exp(a_log)
    lanes = 128
    groups = total_inner // lanes
    inner_f = inner_tok.astype(jnp.float32)
    into = proj[:, RANK : RANK + STATE].reshape(-1)
    outof = proj[:, RANK + STATE :].reshape(-1)
    rate_l = delta_tok.reshape(rows, groups, lanes)
    value_l = inner_f.reshape(rows, groups, lanes)
    decay_l = decay.reshape(state_count, groups, lanes)
    skip_l = skip_gain.reshape(groups, lanes)
    end_l, total_l = run_scan(
        False, into, outof, rate_l, value_l, decay_l,
        jnp.zeros((state_count, groups, lanes), jnp.float32), skip_l,
    )
    pair = jnp.concatenate(
        (end_l.reshape(state_count, total_inner), total_l.reshape(1, total_inner))
    ).reshape(state_count + 1, seq_count, width)
    pair_ch = lax.all_to_all(
        jnp.swapaxes(pair, 0, 1), seq, split_axis=0, concat_axis=0, tiled=True
    )
    decay_ch = lax.dynamic_slice_in_dim(decay, seq_index * width, width, 1)
    carry_ch, carry = run_combine(pair_ch, decay_ch)
    carry_in = lax.all_to_all(carry_ch, seq, split_axis=0, concat_axis=0, tiled=True)
    carry_in = jnp.swapaxes(carry_in, 0, 1).reshape(state_count, total_inner)
    out_l = run_scan(
        True, into, outof, rate_l, value_l, decay_l,
        carry_in.reshape(state_count, groups, lanes), skip_l,
    )
    scanned = out_l.reshape(rows, rows_n, cols_n, width).astype(jnp.bfloat16)
    scanned_grid = lax.all_to_all(scanned, "sy", split_axis=2, concat_axis=0, tiled=True)
    z_here = z_grid.reshape(rows_n, cols_n, rows, width).transpose(1, 2, 0, 3)
    gated = (
        scanned_grid.reshape(cols_n, rows, rows_n, width).astype(jnp.float32)
        * jax.nn.silu(z_here.astype(jnp.float32))
    ).astype(jnp.bfloat16)
    partial = jnp.einsum(
        "ktac,acd->ktd", gated, w_col, preferred_element_type=jnp.float32
    ).astype(jnp.bfloat16)
    branch = lax.psum_scatter(
        partial.reshape(cols_n * rows, model), "sy", scatter_dimension=0, tiled=True
    ).astype(jnp.float32)
    slot_all = gather_a2a(carry[None], ("rx", "rc"), 0)
    picked = (slot_request == req_index).astype(jnp.float32)
    final_state = jnp.sum(picked[:, None, None] * slot_all, axis=0, keepdims=True)
    mixed = (tokens + branch).astype(jnp.bfloat16)[None]
    return (mixed, final_state)


def solution(mesh):
    seq_n = mesh.shape["seq"]
    rows_n = 1
    while rows_n * rows_n < seq_n:
        rows_n *= 2
    grid = Mesh(
        mesh.devices.reshape(mesh.shape["req"] // 2, 2, rows_n, seq_n // rows_n),
        ("rx", "rc", "sz", "sy"),
    )
    req = ("rx", "rc")
    seq = ("sz", "sy")
    in_specs = (
        P(req, seq, None),
        P(),
        P(),
        P(),
        P(None, req, seq),
        P(None, seq),
        P(seq),
        P(seq, None),
        P(None, seq),
        P(seq),
        P(),
        P(),
        P(seq, req),
    )
    out_specs = (P(req, seq, None), P(req, None, seq))
    return jax.shard_map(
        per_device, mesh=grid, in_specs=in_specs, out_specs=out_specs, check_vma=False
    )
```

```python
import functools

import jax
import jax.numpy as jnp
from jax import lax
from jax.experimental import pallas as pl
from jax.experimental.pallas import tpu as pltpu
from jax.sharding import Mesh, PartitionSpec as P

STATE = 16
RANK = 128


def gather_a2a(block, axis, dim):
    count = lax.axis_size(axis)
    copies = jnp.broadcast_to(block[None], (count,) + block.shape)
    stacked = lax.all_to_all(copies, axis, split_axis=0, concat_axis=0, tiled=True)
    moved = jnp.moveaxis(stacked, 0, dim)
    shape = list(block.shape)
    shape[dim] = shape[dim] * count
    return moved.reshape(shape)


LANES = 128
SUB = 8


def scan_body(emit, into_ref, outof_ref, rate_ref, value_ref, decay_ref, start_ref, skip_ref, *outs):
    steps = rate_ref.shape[0]
    states = decay_ref.shape[0]
    decay = [decay_ref[n] for n in range(states)]
    if emit:
        out_ref, = outs
        skip = skip_ref[...]
    else:
        end_ref, total_ref = outs

    def step(t, carry):
        held, acc = carry
        rate = rate_ref[t]
        value = value_ref[t]
        push = rate * value
        row = t * states
        new = []
        result = skip * value if emit else None
        for n in range(states):
            s = jnp.exp(rate * decay[n]) * held[n] + push * into_ref[row + n]
            if emit:
                result = result + outof_ref[row + n] * s
            new.append(s)
        if emit:
            out_ref[t] = result
        else:
            acc = acc + rate
        return (tuple(new), acc)

    held0 = tuple(start_ref[n] for n in range(states))
    acc0 = jnp.zeros((SUB, LANES), jnp.float32)
    held, acc = lax.fori_loop(0, steps, step, (held0, acc0), unroll=4)
    if not emit:
        for n in range(states):
            end_ref[n] = held[n]
        total_ref[0] = acc


def run_scan(emit, into, outof, rate, value, decay, start, skip):
    steps, rows, lanes = rate.shape
    states = decay.shape[0]
    chunks = rows // SUB
    smem = pl.BlockSpec(memory_space=pltpu.MemorySpace.SMEM)
    seq_spec = pl.BlockSpec((steps, SUB, lanes), lambda i: (0, i, 0))
    st_spec = pl.BlockSpec((states, SUB, lanes), lambda i: (0, i, 0))
    skip_spec = pl.BlockSpec((SUB, lanes), lambda i: (i, 0))
    if emit:
        out_shape = jax.ShapeDtypeStruct((steps, rows, lanes), jnp.float32)
        out_specs = seq_spec
    else:
        out_shape = (
            jax.ShapeDtypeStruct((states, rows, lanes), jnp.float32),
            jax.ShapeDtypeStruct((1, rows, lanes), jnp.float32),
        )
        out_specs = (st_spec, pl.BlockSpec((1, SUB, lanes), lambda i: (0, i, 0)))
    flops = steps * rows * lanes * states * 6
    return pl.pallas_call(
        functools.partial(scan_body, emit),
        grid=(chunks,),
        in_specs=[smem, smem, seq_spec, seq_spec, st_spec, st_spec, skip_spec],
        out_specs=out_specs,
        out_shape=out_shape,
        cost_estimate=pl.CostEstimate(
            flops=flops,
            transcendentals=steps * rows * lanes * states,
            bytes_accessed=(3 if emit else 2) * steps * rows * lanes * 4,
        ),
    )(into, outof, rate, value, decay, start, skip)


def combine_body(pair_ref, decay_ref, carries_ref, final_ref):
    blocks = pair_ref.shape[0]
    states = decay_ref.shape[0]
    decay = decay_ref[...]
    carry = jnp.zeros(decay.shape, jnp.float32)
    for block in range(blocks):
        carries_ref[block] = carry
        rows = pair_ref[block]
        carry = jnp.exp(rows[states : states + 1] * decay) * carry + rows[:states]
    final_ref[...] = carry


def run_combine(pair, decay):
    blocks = pair.shape[0]
    states, width = decay.shape
    vmem = pl.BlockSpec(memory_space=pltpu.MemorySpace.VMEM)
    return pl.pallas_call(
        combine_body,
        in_specs=[vmem, vmem],
        out_specs=(vmem, vmem),
        out_shape=(
            jax.ShapeDtypeStruct((blocks, states, width), jnp.float32),
            jax.ShapeDtypeStruct((states, width), jnp.float32),
        ),
    )(pair, decay)


def per_device(
    hidden,
    lengths,
    slot_request,
    norm_gain,
    in_weight,
    conv_weight,
    conv_bias,
    xproj_weight,
    dt_weight,
    dt_bias,
    a_log,
    skip_gain,
    out_weight,
):
    seq = ("sz", "sy")
    rows_n = lax.axis_size("sz")
    cols_n = lax.axis_size("sy")
    seq_count = rows_n * cols_n
    seq_index = lax.axis_index(seq)
    req_index = lax.axis_index(("rx", "rc"))
    rows = hidden.shape[1]
    span = rows * seq_count
    width = in_weight.shape[2]
    taps_count = conv_weight.shape[0]
    state_count = a_log.shape[0]
    total_inner = a_log.shape[1]
    model = hidden.shape[2]
    tokens = hidden[0].astype(jnp.float32)
    scale = lax.rsqrt(jnp.mean(tokens * tokens, axis=-1, keepdims=True) + 1e-05)
    normed = (tokens * scale * norm_gain.astype(jnp.float32)).astype(jnp.bfloat16)
    normed_all = lax.all_gather(normed, seq, axis=0, tiled=True)
    pieces = jnp.concatenate((in_weight, out_weight.T[None]), axis=0)
    pieces_row = gather_a2a(pieces[None], "rx", 0)
    pieces_pair = gather_a2a(pieces_row[None], "rc", 0)
    pieces_all = jnp.moveaxis(
        jnp.swapaxes(pieces_pair, 0, 1).reshape((-1,) + pieces.shape), 0, 1
    ).reshape((pieces.shape[0], -1) + pieces.shape[2:])
    w_in = pieces_all[:2]
    w_out_t = pieces_all[2]
    xproj_w, dt_w, dt_b, _ = lax.optimization_barrier((xproj_weight, dt_weight, dt_bias, normed))
    proj_cols = xproj_w.shape[1]
    small = jnp.concatenate((xproj_w.T, dt_w, dt_b[None]), axis=0)
    lane_half = width // 2
    core = lax.axis_index("rc")
    mine = lax.dynamic_slice_in_dim(small, core * lane_half, lane_half, 1)
    copies = jnp.broadcast_to(mine[None], (seq_count,) + mine.shape)
    half_all = lax.all_to_all(copies, seq, split_axis=0, concat_axis=0, tiled=True)
    both_halves = gather_a2a(half_all[None], "rc", 0)
    small_all = jnp.moveaxis(both_halves, 0, 2).reshape(half_all.shape[:2] + (width,))
    xproj_full = jnp.swapaxes(small_all[:, :proj_cols], 1, 2).reshape(total_inner, proj_cols)
    dt_full = jnp.swapaxes(small_all[:, proj_cols : proj_cols + RANK], 0, 1).reshape(
        RANK, total_inner
    )
    dt_bias_full = small_all[:, proj_cols + RANK].reshape(total_inner)
    w_in, xproj_full, dt_full, dt_bias_full = lax.optimization_barrier(
        (w_in, xproj_full, dt_full, dt_bias_full)
    )
    xin = jnp.dot(normed_all, w_in[0], preferred_element_type=jnp.float32)
    w_late, _ = lax.optimization_barrier((w_out_t, normed_all))
    w_col = lax.all_gather(w_late.T, "sz", axis=0, tiled=False)
    zgate = jnp.dot(normed_all, w_in[1], preferred_element_type=jnp.float32).astype(jnp.bfloat16)
    z_grid = lax.all_to_all(
        zgate.reshape(rows_n, span // rows_n, width), "sz", split_axis=0, concat_axis=0, tiled=True
    )
    padded = jnp.pad(xin, ((taps_count - 1, 0), (0, 0)))
    taps = conv_weight.astype(jnp.float32)
    convolved = conv_bias.astype(jnp.float32) + jnp.zeros_like(xin)
    for tap in range(taps_count):
        convolved = convolved + taps[tap] * padded[tap : tap + span, :]
    inner = jax.nn.silu(convolved).astype(jnp.bfloat16)
    inner_tok = lax.all_to_all(inner, seq, split_axis=0, concat_axis=1, tiled=True)
    proj = jnp.dot(inner_tok, xproj_full, preferred_element_type=jnp.float32)
    length_here = lax.dynamic_index_in_dim(lengths, req_index, 0, keepdims=False)
    positions = seq_index * rows + jnp.arange(rows, dtype=jnp.int32)
    live = (positions < length_here).astype(jnp.float32)
    rate_low = proj[:, :RANK].astype(jnp.bfloat16)
    delta_tok = (
        jax.nn.softplus(
            jnp.dot(rate_low, dt_full, preferred_element_type=jnp.float32)
            + dt_bias_full.astype(jnp.float32)
        )
        * live[:, None]
    )
    decay = -jnp.exp(a_log)
    lanes = 128
    groups = total_inner // lanes
    inner_f = inner_tok.astype(jnp.float32)
    into = proj[:, RANK : RANK + STATE].reshape(-1)
    outof = proj[:, RANK + STATE :].reshape(-1)
    rate_l = delta_tok.reshape(rows, groups, lanes)
    value_l = inner_f.reshape(rows, groups, lanes)
    decay_l = decay.reshape(state_count, groups, lanes)
    skip_l = skip_gain.reshape(groups, lanes)
    end_l, total_l = run_scan(
        False, into, outof, rate_l, value_l, decay_l,
        jnp.zeros((state_count, groups, lanes), jnp.float32), skip_l,
    )
    pair = jnp.concatenate(
        (end_l.reshape(state_count, total_inner), total_l.reshape(1, total_inner))
    ).reshape(state_count + 1, seq_count, width)
    pair_ch = lax.all_to_all(
        jnp.swapaxes(pair, 0, 1), seq, split_axis=0, concat_axis=0, tiled=True
    )
    decay_ch = lax.dynamic_slice_in_dim(decay, seq_index * width, width, 1)
    carry_ch, carry = run_combine(pair_ch, decay_ch)
    carry_in = lax.all_to_all(carry_ch, seq, split_axis=0, concat_axis=0, tiled=True)
    carry_in = jnp.swapaxes(carry_in, 0, 1).reshape(state_count, total_inner)
    out_l = run_scan(
        True, into, outof, rate_l, value_l, decay_l,
        carry_in.reshape(state_count, groups, lanes), skip_l,
    )
    scanned = out_l.reshape(rows, rows_n, cols_n, width).astype(jnp.bfloat16)
    scanned_grid = lax.all_to_all(scanned, "sy", split_axis=2, concat_axis=0, tiled=True)
    z_here = z_grid.reshape(rows_n, cols_n, rows, width).transpose(1, 2, 0, 3)
    gated = (
        scanned_grid.reshape(cols_n, rows, rows_n, width).astype(jnp.float32)
        * jax.nn.silu(z_here.astype(jnp.float32))
    ).astype(jnp.bfloat16)
    partial = jnp.einsum(
        "ktac,acd->ktd", gated, w_col, preferred_element_type=jnp.float32
    ).astype(jnp.bfloat16)
    branch = lax.psum_scatter(
        partial.reshape(cols_n * rows, model), "sy", scatter_dimension=0, tiled=True
    ).astype(jnp.float32)
    slot_all = gather_a2a(carry[None], ("rx", "rc"), 0)
    picked = (slot_request == req_index).astype(jnp.float32)
    final_state = jnp.sum(picked[:, None, None] * slot_all, axis=0, keepdims=True)
    mixed = (tokens + branch).astype(jnp.bfloat16)[None]
    return (mixed, final_state)


def solution(mesh):
    seq_n = mesh.shape["seq"]
    rows_n = 1
    while rows_n * rows_n < seq_n:
        rows_n *= 2
    grid = Mesh(
        mesh.devices.reshape(mesh.shape["req"] // 2, 2, rows_n, seq_n // rows_n),
        ("rx", "rc", "sz", "sy"),
    )
    req = ("rx", "rc")
    seq = ("sz", "sy")
    in_specs = (
        P(req, seq, None),
        P(),
        P(),
        P(),
        P(None, req, seq),
        P(None, seq),
        P(seq),
        P(seq, None),
        P(None, seq),
        P(seq),
        P(),
        P(),
        P(seq, req),
    )
    out_specs = (P(req, seq, None), P(req, None, seq))
    return jax.shard_map(
        per_device, mesh=grid, in_specs=in_specs, out_specs=out_specs, check_vma=False
    )
```

```python
import functools

import jax
import jax.numpy as jnp
from jax import lax
from jax.experimental import pallas as pl
from jax.experimental.pallas import tpu as pltpu
from jax.sharding import Mesh, PartitionSpec as P

STATE = 16
RANK = 128


def gather_a2a(block, axis, dim):
    count = lax.axis_size(axis)
    copies = jnp.broadcast_to(block[None], (count,) + block.shape)
    stacked = lax.all_to_all(copies, axis, split_axis=0, concat_axis=0, tiled=True)
    moved = jnp.moveaxis(stacked, 0, dim)
    shape = list(block.shape)
    shape[dim] = shape[dim] * count
    return moved.reshape(shape)


LANES = 128
SUB = 8


def scan_body(emit, into_ref, outof_ref, rate_ref, value_ref, decay_ref, start_ref, skip_ref, *outs):
    steps = rate_ref.shape[0]
    states = decay_ref.shape[0]
    decay = [decay_ref[n] for n in range(states)]
    if emit:
        out_ref, = outs
        skip = skip_ref[...]
    else:
        end_ref, total_ref = outs

    def step(t, carry):
        held, acc = carry
        rate = rate_ref[t]
        value = value_ref[t]
        push = rate * value
        row = t * states
        new = []
        result = skip * value if emit else None
        for n in range(states):
            s = jnp.exp(rate * decay[n]) * held[n] + push * into_ref[row + n]
            if emit:
                result = result + outof_ref[row + n] * s
            new.append(s)
        if emit:
            out_ref[t] = result
        else:
            acc = acc + rate
        return (tuple(new), acc)

    held0 = tuple(start_ref[n] for n in range(states))
    acc0 = jnp.zeros((SUB, LANES), jnp.float32)
    held, acc = lax.fori_loop(0, steps, step, (held0, acc0), unroll=8)
    if not emit:
        for n in range(states):
            end_ref[n] = held[n]
        total_ref[0] = acc


def run_scan(emit, into, outof, rate, value, decay, start, skip):
    steps, rows, lanes = rate.shape
    states = decay.shape[0]
    chunks = rows // SUB
    smem = pl.BlockSpec(memory_space=pltpu.MemorySpace.SMEM)
    seq_spec = pl.BlockSpec((steps, SUB, lanes), lambda i: (0, i, 0))
    st_spec = pl.BlockSpec((states, SUB, lanes), lambda i: (0, i, 0))
    skip_spec = pl.BlockSpec((SUB, lanes), lambda i: (i, 0))
    if emit:
        out_shape = jax.ShapeDtypeStruct((steps, rows, lanes), jnp.float32)
        out_specs = seq_spec
    else:
        out_shape = (
            jax.ShapeDtypeStruct((states, rows, lanes), jnp.float32),
            jax.ShapeDtypeStruct((1, rows, lanes), jnp.float32),
        )
        out_specs = (st_spec, pl.BlockSpec((1, SUB, lanes), lambda i: (0, i, 0)))
    flops = steps * rows * lanes * states * 6
    return pl.pallas_call(
        functools.partial(scan_body, emit),
        grid=(chunks,),
        in_specs=[smem, smem, seq_spec, seq_spec, st_spec, st_spec, skip_spec],
        out_specs=out_specs,
        out_shape=out_shape,
        cost_estimate=pl.CostEstimate(
            flops=flops,
            transcendentals=steps * rows * lanes * states,
            bytes_accessed=(3 if emit else 2) * steps * rows * lanes * 4,
        ),
    )(into, outof, rate, value, decay, start, skip)


def combine_body(pair_ref, decay_ref, carries_ref, final_ref):
    blocks = pair_ref.shape[0]
    states = decay_ref.shape[0]
    decay = decay_ref[...]
    carry = jnp.zeros(decay.shape, jnp.float32)
    for block in range(blocks):
        carries_ref[block] = carry
        rows = pair_ref[block]
        carry = jnp.exp(rows[states : states + 1] * decay) * carry + rows[:states]
    final_ref[...] = carry


def run_combine(pair, decay):
    blocks = pair.shape[0]
    states, width = decay.shape
    vmem = pl.BlockSpec(memory_space=pltpu.MemorySpace.VMEM)
    return pl.pallas_call(
        combine_body,
        in_specs=[vmem, vmem],
        out_specs=(vmem, vmem),
        out_shape=(
            jax.ShapeDtypeStruct((blocks, states, width), jnp.float32),
            jax.ShapeDtypeStruct((states, width), jnp.float32),
        ),
    )(pair, decay)


def per_device(
    hidden,
    lengths,
    slot_request,
    norm_gain,
    in_weight,
    conv_weight,
    conv_bias,
    xproj_weight,
    dt_weight,
    dt_bias,
    a_log,
    skip_gain,
    out_weight,
):
    seq = ("sz", "sy")
    rows_n = lax.axis_size("sz")
    cols_n = lax.axis_size("sy")
    seq_count = rows_n * cols_n
    seq_index = lax.axis_index(seq)
    req_index = lax.axis_index(("rx", "rc"))
    rows = hidden.shape[1]
    span = rows * seq_count
    width = in_weight.shape[2]
    taps_count = conv_weight.shape[0]
    state_count = a_log.shape[0]
    total_inner = a_log.shape[1]
    model = hidden.shape[2]
    tokens = hidden[0].astype(jnp.float32)
    scale = lax.rsqrt(jnp.mean(tokens * tokens, axis=-1, keepdims=True) + 1e-05)
    normed = (tokens * scale * norm_gain.astype(jnp.float32)).astype(jnp.bfloat16)
    normed_all = lax.all_gather(normed, seq, axis=0, tiled=True)
    pieces = jnp.concatenate((in_weight, out_weight.T[None]), axis=0)
    pieces_row = gather_a2a(pieces[None], "rx", 0)
    pieces_pair = gather_a2a(pieces_row[None], "rc", 0)
    pieces_all = jnp.moveaxis(
        jnp.swapaxes(pieces_pair, 0, 1).reshape((-1,) + pieces.shape), 0, 1
    ).reshape((pieces.shape[0], -1) + pieces.shape[2:])
    w_in = pieces_all[:2]
    w_out_t = pieces_all[2]
    xproj_w, dt_w, dt_b, _ = lax.optimization_barrier((xproj_weight, dt_weight, dt_bias, normed))
    proj_cols = xproj_w.shape[1]
    small = jnp.concatenate((xproj_w.T, dt_w, dt_b[None]), axis=0)
    lane_half = width // 2
    core = lax.axis_index("rc")
    mine = lax.dynamic_slice_in_dim(small, core * lane_half, lane_half, 1)
    copies = jnp.broadcast_to(mine[None], (seq_count,) + mine.shape)
    half_all = lax.all_to_all(copies, seq, split_axis=0, concat_axis=0, tiled=True)
    both_halves = gather_a2a(half_all[None], "rc", 0)
    small_all = jnp.moveaxis(both_halves, 0, 2).reshape(half_all.shape[:2] + (width,))
    xproj_full = jnp.swapaxes(small_all[:, :proj_cols], 1, 2).reshape(total_inner, proj_cols)
    dt_full = jnp.swapaxes(small_all[:, proj_cols : proj_cols + RANK], 0, 1).reshape(
        RANK, total_inner
    )
    dt_bias_full = small_all[:, proj_cols + RANK].reshape(total_inner)
    w_in, xproj_full, dt_full, dt_bias_full = lax.optimization_barrier(
        (w_in, xproj_full, dt_full, dt_bias_full)
    )
    w_flat = jnp.concatenate((w_in[0], w_in[1]), axis=1)
    both = jnp.dot(normed_all, w_flat, preferred_element_type=jnp.float32)
    w_late, _ = lax.optimization_barrier((w_out_t, normed_all))
    w_col = lax.all_gather(w_late.T, "sz", axis=0, tiled=False)
    xin = both[:, :width]
    zgate = both[:, width:].astype(jnp.bfloat16)
    z_grid = lax.all_to_all(
        zgate.reshape(rows_n, span // rows_n, width), "sz", split_axis=0, concat_axis=0, tiled=True
    )
    padded = jnp.pad(xin, ((taps_count - 1, 0), (0, 0)))
    taps = conv_weight.astype(jnp.float32)
    convolved = conv_bias.astype(jnp.float32) + jnp.zeros_like(xin)
    for tap in range(taps_count):
        convolved = convolved + taps[tap] * padded[tap : tap + span, :]
    inner = jax.nn.silu(convolved).astype(jnp.bfloat16)
    inner_tok = lax.all_to_all(inner, seq, split_axis=0, concat_axis=1, tiled=True)
    proj = jnp.dot(inner_tok, xproj_full, preferred_element_type=jnp.float32)
    length_here = lax.dynamic_index_in_dim(lengths, req_index, 0, keepdims=False)
    positions = seq_index * rows + jnp.arange(rows, dtype=jnp.int32)
    live = (positions < length_here).astype(jnp.float32)
    rate_low = proj[:, :RANK].astype(jnp.bfloat16)
    delta_tok = (
        jax.nn.softplus(
            jnp.dot(rate_low, dt_full, preferred_element_type=jnp.float32)
            + dt_bias_full.astype(jnp.float32)
        )
        * live[:, None]
    )
    decay = -jnp.exp(a_log)
    lanes = 128
    groups = total_inner // lanes
    inner_f = inner_tok.astype(jnp.float32)
    into = proj[:, RANK : RANK + STATE].reshape(-1)
    outof = proj[:, RANK + STATE :].reshape(-1)
    rate_l = delta_tok.reshape(rows, groups, lanes)
    value_l = inner_f.reshape(rows, groups, lanes)
    decay_l = decay.reshape(state_count, groups, lanes)
    skip_l = skip_gain.reshape(groups, lanes)
    end_l, total_l = run_scan(
        False, into, outof, rate_l, value_l, decay_l,
        jnp.zeros((state_count, groups, lanes), jnp.float32), skip_l,
    )
    pair = jnp.concatenate(
        (end_l.reshape(state_count, total_inner), total_l.reshape(1, total_inner))
    ).reshape(state_count + 1, seq_count, width)
    pair_ch = lax.all_to_all(
        jnp.swapaxes(pair, 0, 1), seq, split_axis=0, concat_axis=0, tiled=True
    )
    decay_ch = lax.dynamic_slice_in_dim(decay, seq_index * width, width, 1)
    carry_ch, carry = run_combine(pair_ch, decay_ch)
    carry_in = lax.all_to_all(carry_ch, seq, split_axis=0, concat_axis=0, tiled=True)
    carry_in = jnp.swapaxes(carry_in, 0, 1).reshape(state_count, total_inner)
    out_l = run_scan(
        True, into, outof, rate_l, value_l, decay_l,
        carry_in.reshape(state_count, groups, lanes), skip_l,
    )
    scanned = out_l.reshape(rows, rows_n, cols_n, width).astype(jnp.bfloat16)
    scanned_grid = lax.all_to_all(scanned, "sy", split_axis=2, concat_axis=0, tiled=True)
    z_here = z_grid.reshape(rows_n, cols_n, rows, width).transpose(1, 2, 0, 3)
    gated = (
        scanned_grid.reshape(cols_n, rows, rows_n, width).astype(jnp.float32)
        * jax.nn.silu(z_here.astype(jnp.float32))
    ).astype(jnp.bfloat16)
    partial = jnp.einsum(
        "ktac,acd->ktd", gated, w_col, preferred_element_type=jnp.float32
    ).astype(jnp.bfloat16)
    branch = lax.psum_scatter(
        partial.reshape(cols_n * rows, model), "sy", scatter_dimension=0, tiled=True
    ).astype(jnp.float32)
    slot_all = gather_a2a(carry[None], ("rx", "rc"), 0)
    picked = (slot_request == req_index).astype(jnp.float32)
    final_state = jnp.sum(picked[:, None, None] * slot_all, axis=0, keepdims=True)
    mixed = (tokens + branch).astype(jnp.bfloat16)[None]
    return (mixed, final_state)


def solution(mesh):
    seq_n = mesh.shape["seq"]
    rows_n = 1
    while rows_n * rows_n < seq_n:
        rows_n *= 2
    grid = Mesh(
        mesh.devices.reshape(mesh.shape["req"] // 2, 2, rows_n, seq_n // rows_n),
        ("rx", "rc", "sz", "sy"),
    )
    req = ("rx", "rc")
    seq = ("sz", "sy")
    in_specs = (
        P(req, seq, None),
        P(),
        P(),
        P(),
        P(None, req, seq),
        P(None, seq),
        P(seq),
        P(seq, None),
        P(None, seq),
        P(seq),
        P(),
        P(),
        P(seq, req),
    )
    out_specs = (P(req, seq, None), P(req, None, seq))
    return jax.shard_map(
        per_device, mesh=grid, in_specs=in_specs, out_specs=out_specs, check_vma=False
    )
```

```python
import functools

import jax
import jax.numpy as jnp
from jax import lax
from jax.experimental import pallas as pl
from jax.experimental.pallas import tpu as pltpu
from jax.sharding import Mesh, PartitionSpec as P

STATE = 16
RANK = 128


def gather_a2a(block, axis, dim):
    count = lax.axis_size(axis)
    copies = jnp.broadcast_to(block[None], (count,) + block.shape)
    stacked = lax.all_to_all(copies, axis, split_axis=0, concat_axis=0, tiled=True)
    moved = jnp.moveaxis(stacked, 0, dim)
    shape = list(block.shape)
    shape[dim] = shape[dim] * count
    return moved.reshape(shape)


LANES = 128
SUB = 8


def scan_body(emit, into_ref, outof_ref, rate_ref, value_ref, decay_ref, start_ref, skip_ref, *outs):
    steps = rate_ref.shape[0]
    states = decay_ref.shape[0]
    decay = [decay_ref[n] for n in range(states)]
    if emit:
        out_ref, = outs
        skip = skip_ref[...]
    else:
        end_ref, total_ref = outs

    def step(t, carry):
        held, acc = carry
        rate = rate_ref[t]
        value = value_ref[t]
        push = rate * value
        row = t * states
        new = []
        result = skip * value if emit else None
        for n in range(states):
            s = jnp.exp(rate * decay[n]) * held[n] + push * into_ref[row + n]
            if emit:
                result = result + outof_ref[row + n] * s
            new.append(s)
        if emit:
            out_ref[t] = result
        else:
            acc = acc + rate
        return (tuple(new), acc)

    held0 = tuple(start_ref[n] for n in range(states))
    acc0 = jnp.zeros((SUB, LANES), jnp.float32)
    held, acc = lax.fori_loop(0, steps, step, (held0, acc0), unroll=16)
    if not emit:
        for n in range(states):
            end_ref[n] = held[n]
        total_ref[0] = acc


def run_scan(emit, into, outof, rate, value, decay, start, skip):
    steps, rows, lanes = rate.shape
    states = decay.shape[0]
    chunks = rows // SUB
    smem = pl.BlockSpec(memory_space=pltpu.MemorySpace.SMEM)
    seq_spec = pl.BlockSpec((steps, SUB, lanes), lambda i: (0, i, 0))
    st_spec = pl.BlockSpec((states, SUB, lanes), lambda i: (0, i, 0))
    skip_spec = pl.BlockSpec((SUB, lanes), lambda i: (i, 0))
    if emit:
        out_shape = jax.ShapeDtypeStruct((steps, rows, lanes), jnp.float32)
        out_specs = seq_spec
    else:
        out_shape = (
            jax.ShapeDtypeStruct((states, rows, lanes), jnp.float32),
            jax.ShapeDtypeStruct((1, rows, lanes), jnp.float32),
        )
        out_specs = (st_spec, pl.BlockSpec((1, SUB, lanes), lambda i: (0, i, 0)))
    flops = steps * rows * lanes * states * 6
    return pl.pallas_call(
        functools.partial(scan_body, emit),
        grid=(chunks,),
        in_specs=[smem, smem, seq_spec, seq_spec, st_spec, st_spec, skip_spec],
        out_specs=out_specs,
        out_shape=out_shape,
        cost_estimate=pl.CostEstimate(
            flops=flops,
            transcendentals=steps * rows * lanes * states,
            bytes_accessed=(3 if emit else 2) * steps * rows * lanes * 4,
        ),
    )(into, outof, rate, value, decay, start, skip)


def combine_body(pair_ref, decay_ref, carries_ref, final_ref):
    blocks = pair_ref.shape[0]
    states = decay_ref.shape[0]
    decay = decay_ref[...]
    carry = jnp.zeros(decay.shape, jnp.float32)
    for block in range(blocks):
        carries_ref[block] = carry
        rows = pair_ref[block]
        carry = jnp.exp(rows[states : states + 1] * decay) * carry + rows[:states]
    final_ref[...] = carry


def run_combine(pair, decay):
    blocks = pair.shape[0]
    states, width = decay.shape
    vmem = pl.BlockSpec(memory_space=pltpu.MemorySpace.VMEM)
    return pl.pallas_call(
        combine_body,
        in_specs=[vmem, vmem],
        out_specs=(vmem, vmem),
        out_shape=(
            jax.ShapeDtypeStruct((blocks, states, width), jnp.float32),
            jax.ShapeDtypeStruct((states, width), jnp.float32),
        ),
    )(pair, decay)


def per_device(
    hidden,
    lengths,
    slot_request,
    norm_gain,
    in_weight,
    conv_weight,
    conv_bias,
    xproj_weight,
    dt_weight,
    dt_bias,
    a_log,
    skip_gain,
    out_weight,
):
    seq = ("sz", "sy")
    rows_n = lax.axis_size("sz")
    cols_n = lax.axis_size("sy")
    seq_count = rows_n * cols_n
    seq_index = lax.axis_index(seq)
    req_index = lax.axis_index(("rx", "rc"))
    rows = hidden.shape[1]
    span = rows * seq_count
    width = in_weight.shape[2]
    taps_count = conv_weight.shape[0]
    state_count = a_log.shape[0]
    total_inner = a_log.shape[1]
    model = hidden.shape[2]
    tokens = hidden[0].astype(jnp.float32)
    scale = lax.rsqrt(jnp.mean(tokens * tokens, axis=-1, keepdims=True) + 1e-05)
    normed = (tokens * scale * norm_gain.astype(jnp.float32)).astype(jnp.bfloat16)
    normed_all = lax.all_gather(normed, seq, axis=0, tiled=True)
    pieces = jnp.concatenate((in_weight, out_weight.T[None]), axis=0)
    pieces_row = gather_a2a(pieces[None], "rx", 0)
    pieces_pair = gather_a2a(pieces_row[None], "rc", 0)
    pieces_all = jnp.moveaxis(
        jnp.swapaxes(pieces_pair, 0, 1).reshape((-1,) + pieces.shape), 0, 1
    ).reshape((pieces.shape[0], -1) + pieces.shape[2:])
    w_in = pieces_all[:2]
    w_out_t = pieces_all[2]
    xproj_w, dt_w, dt_b, _ = lax.optimization_barrier((xproj_weight, dt_weight, dt_bias, normed))
    proj_cols = xproj_w.shape[1]
    small = jnp.concatenate((xproj_w.T, dt_w, dt_b[None]), axis=0)
    lane_half = width // 2
    core = lax.axis_index("rc")
    mine = lax.dynamic_slice_in_dim(small, core * lane_half, lane_half, 1)
    copies = jnp.broadcast_to(mine[None], (seq_count,) + mine.shape)
    half_all = lax.all_to_all(copies, seq, split_axis=0, concat_axis=0, tiled=True)
    both_halves = gather_a2a(half_all[None], "rc", 0)
    small_all = jnp.moveaxis(both_halves, 0, 2).reshape(half_all.shape[:2] + (width,))
    xproj_full = jnp.swapaxes(small_all[:, :proj_cols], 1, 2).reshape(total_inner, proj_cols)
    dt_full = jnp.swapaxes(small_all[:, proj_cols : proj_cols + RANK], 0, 1).reshape(
        RANK, total_inner
    )
    dt_bias_full = small_all[:, proj_cols + RANK].reshape(total_inner)
    w_in, xproj_full, dt_full, dt_bias_full = lax.optimization_barrier(
        (w_in, xproj_full, dt_full, dt_bias_full)
    )
    w_flat = jnp.concatenate((w_in[0], w_in[1]), axis=1)
    both = jnp.dot(normed_all, w_flat, preferred_element_type=jnp.float32)
    w_late, _ = lax.optimization_barrier((w_out_t, normed_all))
    w_col = lax.all_gather(w_late.T, "sz", axis=0, tiled=False)
    xin = both[:, :width]
    zgate = both[:, width:].astype(jnp.bfloat16)
    z_grid = lax.all_to_all(
        zgate.reshape(rows_n, span // rows_n, width), "sz", split_axis=0, concat_axis=0, tiled=True
    )
    padded = jnp.pad(xin, ((taps_count - 1, 0), (0, 0)))
    taps = conv_weight.astype(jnp.float32)
    convolved = conv_bias.astype(jnp.float32) + jnp.zeros_like(xin)
    for tap in range(taps_count):
        convolved = convolved + taps[tap] * padded[tap : tap + span, :]
    inner = jax.nn.silu(convolved).astype(jnp.bfloat16)
    inner_tok = lax.all_to_all(inner, seq, split_axis=0, concat_axis=1, tiled=True)
    proj = jnp.dot(inner_tok, xproj_full, preferred_element_type=jnp.float32)
    length_here = lax.dynamic_index_in_dim(lengths, req_index, 0, keepdims=False)
    positions = seq_index * rows + jnp.arange(rows, dtype=jnp.int32)
    live = (positions < length_here).astype(jnp.float32)
    rate_low = proj[:, :RANK].astype(jnp.bfloat16)
    delta_tok = (
        jax.nn.softplus(
            jnp.dot(rate_low, dt_full, preferred_element_type=jnp.float32)
            + dt_bias_full.astype(jnp.float32)
        )
        * live[:, None]
    )
    decay = -jnp.exp(a_log)
    lanes = 128
    groups = total_inner // lanes
    inner_f = inner_tok.astype(jnp.float32)
    into = proj[:, RANK : RANK + STATE].reshape(-1)
    outof = proj[:, RANK + STATE :].reshape(-1)
    rate_l = delta_tok.reshape(rows, groups, lanes)
    value_l = inner_f.reshape(rows, groups, lanes)
    decay_l = decay.reshape(state_count, groups, lanes)
    skip_l = skip_gain.reshape(groups, lanes)
    end_l, total_l = run_scan(
        False, into, outof, rate_l, value_l, decay_l,
        jnp.zeros((state_count, groups, lanes), jnp.float32), skip_l,
    )
    pair = jnp.concatenate(
        (end_l.reshape(state_count, total_inner), total_l.reshape(1, total_inner))
    ).reshape(state_count + 1, seq_count, width)
    pair_ch = lax.all_to_all(
        jnp.swapaxes(pair, 0, 1), seq, split_axis=0, concat_axis=0, tiled=True
    )
    decay_ch = lax.dynamic_slice_in_dim(decay, seq_index * width, width, 1)
    carry_ch, carry = run_combine(pair_ch, decay_ch)
    carry_in = lax.all_to_all(carry_ch, seq, split_axis=0, concat_axis=0, tiled=True)
    carry_in = jnp.swapaxes(carry_in, 0, 1).reshape(state_count, total_inner)
    out_l = run_scan(
        True, into, outof, rate_l, value_l, decay_l,
        carry_in.reshape(state_count, groups, lanes), skip_l,
    )
    scanned = out_l.reshape(rows, rows_n, cols_n, width).astype(jnp.bfloat16)
    scanned_grid = lax.all_to_all(scanned, "sy", split_axis=2, concat_axis=0, tiled=True)
    z_here = z_grid.reshape(rows_n, cols_n, rows, width).transpose(1, 2, 0, 3)
    gated = (
        scanned_grid.reshape(cols_n, rows, rows_n, width).astype(jnp.float32)
        * jax.nn.silu(z_here.astype(jnp.float32))
    ).astype(jnp.bfloat16)
    partial = jnp.einsum(
        "ktac,acd->ktd", gated, w_col, preferred_element_type=jnp.float32
    ).astype(jnp.bfloat16)
    branch = lax.psum_scatter(
        partial.reshape(cols_n * rows, model), "sy", scatter_dimension=0, tiled=True
    ).astype(jnp.float32)
    slot_all = gather_a2a(carry[None], ("rx", "rc"), 0)
    picked = (slot_request == req_index).astype(jnp.float32)
    final_state = jnp.sum(picked[:, None, None] * slot_all, axis=0, keepdims=True)
    mixed = (tokens + branch).astype(jnp.bfloat16)[None]
    return (mixed, final_state)


def solution(mesh):
    seq_n = mesh.shape["seq"]
    rows_n = 1
    while rows_n * rows_n < seq_n:
        rows_n *= 2
    grid = Mesh(
        mesh.devices.reshape(mesh.shape["req"] // 2, 2, rows_n, seq_n // rows_n),
        ("rx", "rc", "sz", "sy"),
    )
    req = ("rx", "rc")
    seq = ("sz", "sy")
    in_specs = (
        P(req, seq, None),
        P(),
        P(),
        P(),
        P(None, req, seq),
        P(None, seq),
        P(seq),
        P(seq, None),
        P(None, seq),
        P(seq),
        P(),
        P(),
        P(seq, req),
    )
    out_specs = (P(req, seq, None), P(req, None, seq))
    return jax.shard_map(
        per_device, mesh=grid, in_specs=in_specs, out_specs=out_specs, check_vma=False
    )
```
